512 devices in a mesh: region: 4 (over z_lo), gx: 16 (over y, z_hi), gy: 8 (over x, core).
Axes of the slice: x: 4, y: 8, z: 8 (z_hi: 2, z_lo: 4; z = z_hi * 4 + z_lo), core: 2. Of those that a mesh axis runs over, the one named last changes fastest.
Arguments:
- spins: float32 [3, 8, 512, 1024], P(None, 'region', 'gx', 'gy'), may hold values from -1 to 1, as said below
- uniforms: float32 [2, 8, 512, 1024], P(None, 'region', 'gx', 'gy'), may hold values from 0 to 1
- trials: float32 [2, 3, 8, 512, 1024], P(None, None, 'region', 'gx', 'gy'), may hold values from -1 to 1
- exch_kernel: float32 [3, 3, 3], replicated, may hold values from -0.5 to 1
- film_m: float32 [3, 8192, 2048], P(None, ('region', 'gx'), 'gy'), may hold values from -1 to 1, as said below
- film_anis: float32 [8192, 2048], P(('region', 'gx'), 'gy'), may hold values from 0.2 to 2
Outputs:
- spins_out: float32 [3, 8, 512, 1024], P(None, 'region', 'gx', 'gy')
- film_out: float32 [3, 8192, 2048], P(None, ('region', 'gx'), 'gy')
The draws below stay inside these ranges and needn't reach their ends.
Inputs may be any that keep to these rules, and one draw needn't show every extreme that they name: `spins`: the three components of each site form a unit vector. `film_m`: the three components of each cell form a unit vector.
All inputs are finite; a program needn't handle non-finite values.
Results may differ from the reference program's by a relative error of at most 0.0001.
Values sent between devices are 32-bit elements; how exact they have to be, the bound alone decides.
No kernel may reach another device: no remote copies, remote signals or barrier semaphores. Data moves between devices by JAX's collectives and lax.ppermute only.
A program may use at most 64 MiB of HBM per device.

```python
import math
import jax
import jax.numpy as jnp
from jax import lax

K = 8
SWEEPS = 2
AL = 8
AX = 512
AY = 1024
FX = 8192
FY = 2048


def unit_field(key, shape):
    first_key, second_key = jax.random.split(key)
    height = jax.random.uniform(first_key, shape, jnp.float32, -1.0, 1.0)
    azimuth = jax.random.uniform(second_key, shape, jnp.float32, -math.pi, math.pi)
    radius = jnp.sqrt(jnp.maximum(1.0 - height * height, 0.0))
    return jnp.stack([radius * jnp.cos(azimuth), radius * jnp.sin(azimuth), height])


def draw_spins(key, part):
    return unit_field(jax.random.fold_in(key, 11), (AL, AX, AY))


def draw_film_m(key, part):
    return unit_field(jax.random.fold_in(key, 23), (FX, FY))


def level_of(stream_key, extent, shards, least, largest):
    loudness, own = 1.0, jax.random.fold_in(stream_key, 6)
    for axis_at, parts in shards:
        draws = jnp.exp(jax.random.uniform(jax.random.fold_in(own, axis_at), (parts,), jnp.float32, least / len(shards), largest / len(shards)))
        loudness = loudness * jnp.repeat(draws, extent[axis_at] // parts).reshape([-1 if axis == axis_at else 1 for axis in range(len(extent))])
    return loudness


def setup_inputs(seed: int = 0) -> dict:
    keys = jax.random.split(jax.random.key(seed), 7)
    spins = draw_spins(jax.random.fold_in(keys[6], 71), 0)
    uniforms = jnp.clip(1.0 * jax.random.uniform(keys[1], (SWEEPS, AL, AX, AY), jnp.float32) ** level_of(keys[1], (SWEEPS, AL, AX, AY), ((1, 4), (2, 16), (3, 8)), -0.2, 0.2), 0.0, 1.0)
    trials = jnp.clip(jax.random.uniform(keys[2], (SWEEPS, 3, AL, AX, AY), jnp.float32, -1.0, 1.0) * level_of(keys[2], (SWEEPS, 3, AL, AX, AY), ((2, 4), (3, 16), (4, 8)), -0.4, 0.0), -1.0, 1.0)
    exch_kernel = jnp.clip(jax.random.uniform(keys[3], (3, 3, 3), jnp.float32, -0.5, 1.0), -0.5, 1.0)
    film_m = draw_film_m(jax.random.fold_in(keys[6], 71), 0)
    film_anis = jnp.clip(jnp.exp(math.log(2.0) - 2.3025851 * jax.random.uniform(keys[5], (FX, FY), jnp.float32) ** level_of(keys[5], (FX, FY), ((0, 64), (1, 8)), -0.2, 0.2)), 0.2, 2.0)
    return {"spins": spins, "uniforms": uniforms, "trials": trials, "exch_kernel": exch_kernel, "film_m": film_m, "film_anis": film_anis}


coupling_down = 1.0
anisotropy = 0.5
inverse_temp = 2.0
softness = 0.05
step_cone = 0.4
coupling_up = 2.0
damping = 0.1
time_step = 0.05

def normalized(vector):
    return vector / jnp.sqrt(lax.optimization_barrier(jnp.sum(vector * vector, axis=0, keepdims=True)))

def apply_kernel(matrix, vector):
    return jnp.stack([matrix[component, 0] * vector[0] + matrix[component, 1] * vector[1] + matrix[component, 2] * vector[2] for component in range(3)])

def apply_transposed(matrix, vector):
    return jnp.stack([matrix[0, component] * vector[0] + matrix[1, component] * vector[1] + matrix[2, component] * vector[2] for component in range(3)])

def local_field(padded, exch_kernel):
    forward = (padded[:, 2:, 1:-1, 1:-1], padded[:, 1:-1, 2:, 1:-1], padded[:, 1:-1, 1:-1, 2:])
    backward = (padded[:, :-2, 1:-1, 1:-1], padded[:, 1:-1, :-2, 1:-1], padded[:, 1:-1, 1:-1, :-2])
    summed = apply_kernel(exch_kernel[0], forward[0]) + apply_transposed(exch_kernel[0], backward[0])
    for direction in (1, 2):
        summed = summed + apply_kernel(exch_kernel[direction], forward[direction])
        summed = summed + apply_transposed(exch_kernel[direction], backward[direction])
    return summed

def metropolis(spins, padded, exch_kernel, film_near, trial_move, uniform_draw, colour_mask):
    field_sum = local_field(padded, exch_kernel) + coupling_down * film_near
    proposal = normalized(spins + step_cone * trial_move)
    change = -lax.optimization_barrier(jnp.sum((proposal - spins) * field_sum, axis=0)) - anisotropy * (proposal[2] * proposal[2] - spins[2] * spins[2])
    accept = jnp.exp(jnp.minimum(-inverse_temp * change, 0.0))
    weight = jax.nn.sigmoid((accept - uniform_draw) / softness)
    blended = normalized((1.0 - weight) * spins + weight * proposal)
    return jnp.where(colour_mask[None], blended, spins)

def cross_product(left, right):
    return jnp.stack([left[1] * right[2] - left[2] * right[1], left[2] * right[0] - left[0] * right[2], left[0] * right[1] - left[1] * right[0]])

def film_rate(magnet, padded, film_anis, interface):
    laplace_sum = padded[:, 2:, 1:-1] + padded[:, :-2, 1:-1] + padded[:, 1:-1, 2:] + padded[:, 1:-1, :-2] - 4.0 * magnet
    field_sum = laplace_sum + coupling_up * interface
    field_sum = jnp.stack([field_sum[0], field_sum[1], field_sum[2] + film_anis * magnet[2]])
    precession = cross_product(magnet, field_sum)
    relaxation = cross_product(magnet, precession)
    return -(precession + damping * relaxation) / (1.0 + damping * damping)

def reference(spins, uniforms, trials, exch_kernel, film_m, film_anis):
    cells_x = AX // K
    cells_y = AY // K
    film_block = film_m[:, :cells_x, :cells_y]
    film_cells = jnp.repeat(jnp.repeat(film_block, K, axis=1), K, axis=2)
    layer_pos = jnp.arange(AL, dtype=jnp.int32)
    film_near = jnp.broadcast_to(film_cells[:, None], (3, AL, AX, AY))
    parity = (layer_pos[:, None, None] + jnp.arange(AX, dtype=jnp.int32)[None, :, None] + jnp.arange(AY, dtype=jnp.int32)[None, None, :]) % 2
    for sweep_index in range(SWEEPS):
        for colour in (0, 1):
            padded = jnp.pad(spins, ((0, 0), (1, 1), (1, 1), (1, 1)))
            spins = metropolis(spins, padded, exch_kernel, film_near, trials[sweep_index], uniforms[sweep_index], parity == colour)
    averages = spins[:, 0].reshape(3, cells_x, K, cells_y, K).mean(axis=(2, 4))
    interface = jnp.pad(averages, ((0, 0), (0, FX - cells_x), (0, FY - cells_y)))
    rate_start = film_rate(film_m, jnp.pad(film_m, ((0, 0), (1, 1), (1, 1))), film_anis, interface)
    predicted = film_m + time_step * rate_start
    rate_trial = film_rate(predicted, jnp.pad(predicted, ((0, 0), (1, 1), (1, 1))), film_anis, interface)
    corrected = film_m + 0.5 * time_step * (rate_start + rate_trial)
    return (spins, normalized(corrected))
```

```python
import functools

import jax
import jax.numpy as jnp
from jax import lax
from jax.sharding import Mesh
from jax.sharding import PartitionSpec as P
from jax.experimental import pallas as pl
from jax.experimental.pallas import tpu as pltpu

K = 8
SWEEPS = 2
REGION_GX = ("region", "gx_0", "gx_1")
GY = ("gy_0", "gy_1")
GX = ("gx_0", "gx_1")


coupling_down = 1.0
anisotropy = 0.5
inverse_temp = 2.0
softness = 0.05
step_cone = 0.4
coupling_up = 2.0
damping = 0.1
time_step = 0.05


def with_halo(array, sides, width):
    edges = {}
    for axis, dim in sides:
        count, length = (lax.axis_size(axis), array.shape[dim])
        up = [(i, (i + 1) % count) for i in range(count - 1)]
        last = lax.slice_in_dim(array, length - width, length, axis=dim)
        leading = lax.slice_in_dim(array, 0, width, axis=dim)
        edges[dim] = (
            lax.ppermute(last, axis, up),
            lax.ppermute(leading, axis, [(b, a) for a, b in up]),
        )
    done = []
    for _, dim in sides:
        low, high = edges[dim]
        around = [(width, width) if d in done else (0, 0) for d in range(array.ndim)]
        array = jnp.concatenate([jnp.pad(low, around), array, jnp.pad(high, around)], axis=dim)
        done.append(dim)
    return array


def split_up(array, dim, count):
    shape = array.shape
    parts = array.reshape(*shape[:dim], count, shape[dim] // count, *shape[dim + 1 :])
    return jnp.moveaxis(parts, dim, 0)


def summed_on_arrival(array, axis, dim):
    parts = split_up(array, dim, lax.axis_size(axis))
    arrived = lax.all_to_all(parts, axis, split_axis=0, concat_axis=0, tiled=True)
    return arrived.sum(axis=0)


def summed_rows(array, axes, dim):
    far, near = axes
    own = summed_on_arrival(split_up(array, dim, lax.axis_size(far)), near, dim + 1)
    return jnp.sum(lax.all_to_all(own, far, 0, 0, tiled=True), axis=0)


def picked(array, axis, root):
    return lax.dynamic_index_in_dim(lax.all_gather(array, axis), root, 0, keepdims=False)


def copy_for_each(array, axis):
    count = lax.axis_size(axis)
    return lax.all_to_all(
        jnp.broadcast_to(array[None], (count, *array.shape)), axis, 0, 0, tiled=True
    )


def laid_out(parts, dim):
    shape = list(parts.shape[1:])
    shape[dim] *= parts.shape[0]
    return jnp.moveaxis(parts, 0, dim).reshape(shape)


def whole_of(array, axes, dim):
    far, near = axes
    parts = copy_for_each(copy_for_each(array, far), near)
    return laid_out(parts.swapaxes(0, 1).reshape(-1, *array.shape), dim)


def normalized(vector):
    return vector / jnp.sqrt(jnp.sum(vector * vector, axis=0, keepdims=True))


def apply_kernel(matrix, vector):
    return jnp.stack(
        [
            matrix[component, 0] * vector[0]
            + matrix[component, 1] * vector[1]
            + matrix[component, 2] * vector[2]
            for component in range(3)
        ]
    )


def apply_transposed(matrix, vector):
    return jnp.stack(
        [
            matrix[0, component] * vector[0]
            + matrix[1, component] * vector[1]
            + matrix[2, component] * vector[2]
            for component in range(3)
        ]
    )


def local_field(padded, exch_kernel):
    forward = (padded[:, 2:, 1:-1, 1:-1], padded[:, 1:-1, 2:, 1:-1], padded[:, 1:-1, 1:-1, 2:])
    backward = (padded[:, :-2, 1:-1, 1:-1], padded[:, 1:-1, :-2, 1:-1], padded[:, 1:-1, 1:-1, :-2])
    summed = apply_kernel(exch_kernel[0], forward[0]) + apply_transposed(
        exch_kernel[0], backward[0]
    )
    for direction in (1, 2):
        summed = summed + apply_kernel(exch_kernel[direction], forward[direction])
        summed = summed + apply_transposed(exch_kernel[direction], backward[direction])
    return summed


def metropolis(spins, padded, exch_kernel, film_near, trial_move, uniform_draw, colour_mask):
    field_sum = local_field(padded, exch_kernel) + coupling_down * film_near
    proposal = normalized(spins + step_cone * trial_move)
    change = -jnp.sum((proposal - spins) * field_sum, axis=0) - anisotropy * (
        proposal[2] * proposal[2] - spins[2] * spins[2]
    )
    accept = jnp.exp(jnp.minimum(-inverse_temp * change, 0.0))
    weight = jax.nn.sigmoid((accept - uniform_draw) / softness)
    blended = normalized((1.0 - weight) * spins + weight * proposal)
    return jnp.where(colour_mask[None], blended, spins)


def sweep_kernel(colour, sweep, k_ref, s_ref, lo_ref, hi_ref, xlo_ref, xhi_ref, ylo_ref, yhi_ref,
                 film_ref, trial_ref, unif_ref,
                 out_ref, olo_ref, ohi_ref, oxlo_ref, oxhi_ref, oylo_ref, oyhi_ref):
    layers, rows_x, rows_y = s_ref.shape[1:]
    row = lax.broadcasted_iota(jnp.int32, (rows_x, rows_y), 0)
    col = lax.broadcasted_iota(jnp.int32, (rows_x, rows_y), 1)
    kk = [[[k_ref[d * 9 + a * 3 + b] for b in range(3)] for a in range(3)] for d in range(3)]
    for l in range(layers):
        s = [s_ref[c, l] for c in range(3)]
        below = [lo_ref[c, 0] if l == 0 else s_ref[c, l - 1] for c in range(3)]
        above = [hi_ref[c, 0] if l == layers - 1 else s_ref[c, l + 1] for c in range(3)]
        xp = [jnp.where(row == rows_x - 1, xhi_ref[c, l], pltpu.roll(s[c], rows_x - 1, 0)) for c in range(3)]
        xm = [jnp.where(row == 0, xlo_ref[c, l], pltpu.roll(s[c], 1, 0)) for c in range(3)]
        yp = [jnp.where(col == rows_y - 1, yhi_ref[c, l], pltpu.roll(s[c], rows_y - 1, 1)) for c in range(3)]
        ym = [jnp.where(col == 0, ylo_ref[c, l], pltpu.roll(s[c], 1, 1)) for c in range(3)]
        fwd = (above, xp, yp)
        bwd = (below, xm, ym)
        field = []
        for c in range(3):
            total = film_ref[c] * coupling_down
            for d in range(3):
                m = kk[d]
                total = total + (m[c][0] * fwd[d][0] + m[c][1] * fwd[d][1] + m[c][2] * fwd[d][2])
                total = total + (m[0][c] * bwd[d][0] + m[1][c] * bwd[d][1] + m[2][c] * bwd[d][2])
            field.append(total)
        raw = [s[c] + step_cone * trial_ref[sweep, c, l] for c in range(3)]
        norm = jnp.sqrt(raw[0] * raw[0] + raw[1] * raw[1] + raw[2] * raw[2])
        prop = [raw[c] / norm for c in range(3)]
        dot = (prop[0] - s[0]) * field[0] + (prop[1] - s[1]) * field[1] + (prop[2] - s[2]) * field[2]
        change = -dot - anisotropy * (prop[2] * prop[2] - s[2] * s[2])
        accept = jnp.exp(jnp.minimum(-inverse_temp * change, 0.0))
        weight = 1.0 / (1.0 + jnp.exp(-((accept - unif_ref[sweep, l]) / softness)))
        mix = [(1.0 - weight) * s[c] + weight * prop[c] for c in range(3)]
        mnorm = jnp.sqrt(mix[0] * mix[0] + mix[1] * mix[1] + mix[2] * mix[2])
        chosen = ((row + col + l) % 2) == colour
        for c in range(3):
            new = jnp.where(chosen, mix[c] / mnorm, s[c])
            out_ref[c, l] = new
            if l == 0:
                olo_ref[c, 0] = new
            if l == layers - 1:
                ohi_ref[c, 0] = new
            oxlo_ref[c, l] = new[0:1, :]
            oxhi_ref[c, l] = new[rows_x - 1:rows_x, :]
            oylo_ref[c, l] = new[:, 0:1]
            oyhi_ref[c, l] = new[:, rows_y - 1:rows_y]


def half_sweep(spins, halos, exch_flat, film_cells, trials, uniforms, sweep, colour):
    comps, layers, rows_x, rows_y = spins.shape
    vmem = pl.BlockSpec(memory_space=pltpu.VMEM)
    smem = pl.BlockSpec(memory_space=pltpu.SMEM)
    dt = spins.dtype
    out_shape = (
        jax.ShapeDtypeStruct(spins.shape, dt),
        jax.ShapeDtypeStruct((comps, 1, rows_x, rows_y), dt),
        jax.ShapeDtypeStruct((comps, 1, rows_x, rows_y), dt),
        jax.ShapeDtypeStruct((comps, layers, 1, rows_y), dt),
        jax.ShapeDtypeStruct((comps, layers, 1, rows_y), dt),
        jax.ShapeDtypeStruct((comps, layers, rows_x, 1), dt),
        jax.ShapeDtypeStruct((comps, layers, rows_x, 1), dt),
    )
    sites = layers * rows_x * rows_y
    return pl.pallas_call(
        functools.partial(sweep_kernel, colour, sweep),
        out_shape=out_shape,
        in_specs=[smem] + [vmem] * 10,
        out_specs=tuple([vmem] * 7),
        cost_estimate=pl.CostEstimate(flops=200 * sites, transcendentals=4 * sites, bytes_accessed=4 * 14 * sites),
    )(exch_flat, spins, *halos, film_cells, trials, uniforms)


def spin_halos(faces):
    lo, hi, xlo, xhi, ylo, yhi = faces
    out = []
    for axis, low_src, high_src in (("region", hi, lo), (GX, xhi, xlo), (GY, yhi, ylo)):
        count = lax.axis_size(axis)
        up = [(i, i + 1) for i in range(count - 1)]
        out.append(lax.ppermute(low_src, axis, up))
        out.append(lax.ppermute(high_src, axis, [(b, a) for a, b in up]))
    return out


def cross_product(left, right):
    return jnp.stack(
        [
            left[1] * right[2] - left[2] * right[1],
            left[2] * right[0] - left[0] * right[2],
            left[0] * right[1] - left[1] * right[0],
        ]
    )


def film_rate(magnet, padded, film_anis, interface):
    laplace_sum = (
        padded[:, 2:, 1:-1]
        + padded[:, :-2, 1:-1]
        + padded[:, 1:-1, 2:]
        + padded[:, 1:-1, :-2]
        - 4.0 * magnet
    )
    field_sum = laplace_sum + coupling_up * interface
    field_sum = jnp.stack([field_sum[0], field_sum[1], field_sum[2] + film_anis * magnet[2]])
    precession = cross_product(magnet, field_sum)
    relaxation = cross_product(magnet, precession)
    return -(precession + damping * relaxation) / (1.0 + damping * damping)


def film_halo(magnet):
    return with_halo(magnet, ((REGION_GX, 1), (GY, 2)), 1)


def body(spins, uniforms, trials, exch_kernel, film_m, film_anis):
    layers_dev = spins.shape[1]
    rows_x = spins.shape[2]
    rows_y = spins.shape[3]
    piece_x = rows_x // K
    piece_y = rows_y // K
    gx_count = lax.axis_size(GX)
    gy_count = lax.axis_size(GY)
    tile_count = gx_count * gy_count
    region_pos = lax.axis_index("region")
    gx_pos = lax.axis_index(GX)
    gy_pos = lax.axis_index(GY)
    first_tile = (region_pos == 0) & (gx_pos == 0) & (gy_pos == 0)
    film_block = film_m[:, : piece_x * gx_count, : piece_y * gy_count]
    stack_spins, unif_all, trial_all = (spins, uniforms, trials)
    assert layers_dev % 2 == 0 and rows_x % 2 == 0 and rows_y % 2 == 0
    pieces = (
        film_block.reshape(3, gx_count, piece_x, gy_count, piece_y)
        .transpose(1, 3, 0, 2, 4)
        .reshape(tile_count, 3, piece_x, piece_y)
    )
    pieces = jnp.where(first_tile, pieces, 0.0)
    placed = summed_rows(pieces, (("gx_0", "gx_1", "gy_0"), "gy_1"), 0)[0]
    own_cells = picked(placed, "region", 0)
    film_cells = jnp.repeat(jnp.repeat(own_cells, K, axis=1), K, axis=2)
    exch_flat = exch_kernel.reshape(-1)
    faces = (
        stack_spins[:, :1],
        stack_spins[:, -1:],
        stack_spins[:, :, :1],
        stack_spins[:, :, -1:],
        stack_spins[:, :, :, :1],
        stack_spins[:, :, :, -1:],
    )
    for sweep_index in range(SWEEPS):
        for colour in (0, 1):
            halos = spin_halos(faces)
            stack_spins, *faces = half_sweep(
                stack_spins, halos, exch_flat, film_cells, trial_all, unif_all, sweep_index, colour
            )
    averages = stack_spins[:, 0].reshape(3, piece_x, K, piece_y, K).mean(axis=(2, 4))
    gathered = whole_of(averages[None], (("gx_0", "gx_1", "gy_0"), "gy_1"), 0)
    assembled = (
        gathered.reshape(gx_count, gy_count, 3, piece_x, piece_y)
        .transpose(2, 0, 3, 1, 4)
        .reshape(3, gx_count * piece_x, gy_count * piece_y)
    )
    padded_block = jnp.pad(
        assembled,
        (
            (0, 0),
            (0, film_m.shape[1] - assembled.shape[1]),
            (0, film_m.shape[2] - assembled.shape[2]),
        ),
    )
    interface = jnp.where(first_tile, padded_block, 0.0)
    rate_start = film_rate(film_m, film_halo(film_m), film_anis, interface)
    predicted = film_m + time_step * rate_start
    rate_trial = film_rate(predicted, film_halo(predicted), film_anis, interface)
    corrected = film_m + 0.5 * time_step * (rate_start + rate_trial)
    return (stack_spins, normalized(corrected))


def solution(mesh):
    finer = Mesh(
        mesh.devices.reshape(mesh.shape["region"], 8, 2, 4, 2),
        ("region", "gx_0", "gx_1", "gy_0", "gy_1"),
    )
    in_specs = (
        P(None, "region", GX, GY),
        P(None, "region", GX, GY),
        P(None, None, "region", GX, GY),
        P(),
        P(None, REGION_GX, GY),
        P(REGION_GX, GY),
    )
    out_specs = (P(None, "region", GX, GY), P(None, REGION_GX, GY))
    return jax.shard_map(body, mesh=finer, in_specs=in_specs, out_specs=out_specs, check_vma=False)
```

```python
import functools

import jax
import jax.numpy as jnp
from jax import lax
from jax.sharding import Mesh
from jax.sharding import PartitionSpec as P
from jax.experimental import pallas as pl
from jax.experimental.pallas import tpu as pltpu

K = 8
SWEEPS = 2
REGION_GX = ("region", "gx_0", "gx_1")
GY = ("gy_0", "gy_1")
GX = ("gx_0", "gx_1")


coupling_down = 1.0
anisotropy = 0.5
inverse_temp = 2.0
softness = 0.05
step_cone = 0.4
coupling_up = 2.0
damping = 0.1
time_step = 0.05


def with_halo(array, sides, width):
    edges = {}
    for axis, dim in sides:
        count, length = (lax.axis_size(axis), array.shape[dim])
        up = [(i, (i + 1) % count) for i in range(count - 1)]
        last = lax.slice_in_dim(array, length - width, length, axis=dim)
        leading = lax.slice_in_dim(array, 0, width, axis=dim)
        edges[dim] = (
            lax.ppermute(last, axis, up),
            lax.ppermute(leading, axis, [(b, a) for a, b in up]),
        )
    done = []
    for _, dim in sides:
        low, high = edges[dim]
        around = [(width, width) if d in done else (0, 0) for d in range(array.ndim)]
        array = jnp.concatenate([jnp.pad(low, around), array, jnp.pad(high, around)], axis=dim)
        done.append(dim)
    return array


def split_up(array, dim, count):
    shape = array.shape
    parts = array.reshape(*shape[:dim], count, shape[dim] // count, *shape[dim + 1 :])
    return jnp.moveaxis(parts, dim, 0)


def summed_on_arrival(array, axis, dim):
    parts = split_up(array, dim, lax.axis_size(axis))
    arrived = lax.all_to_all(parts, axis, split_axis=0, concat_axis=0, tiled=True)
    return arrived.sum(axis=0)


def summed_rows(array, axes, dim):
    far, near = axes
    own = summed_on_arrival(split_up(array, dim, lax.axis_size(far)), near, dim + 1)
    return jnp.sum(lax.all_to_all(own, far, 0, 0, tiled=True), axis=0)


def picked(array, axis, root):
    return lax.dynamic_index_in_dim(lax.all_gather(array, axis), root, 0, keepdims=False)


def copy_for_each(array, axis):
    count = lax.axis_size(axis)
    return lax.all_to_all(
        jnp.broadcast_to(array[None], (count, *array.shape)), axis, 0, 0, tiled=True
    )


def laid_out(parts, dim):
    shape = list(parts.shape[1:])
    shape[dim] *= parts.shape[0]
    return jnp.moveaxis(parts, 0, dim).reshape(shape)


def whole_of(array, axes, dim):
    far, near = axes
    parts = copy_for_each(copy_for_each(array, far), near)
    return laid_out(parts.swapaxes(0, 1).reshape(-1, *array.shape), dim)


def normalized(vector):
    return vector / jnp.sqrt(jnp.sum(vector * vector, axis=0, keepdims=True))


def apply_kernel(matrix, vector):
    return jnp.stack(
        [
            matrix[component, 0] * vector[0]
            + matrix[component, 1] * vector[1]
            + matrix[component, 2] * vector[2]
            for component in range(3)
        ]
    )


def apply_transposed(matrix, vector):
    return jnp.stack(
        [
            matrix[0, component] * vector[0]
            + matrix[1, component] * vector[1]
            + matrix[2, component] * vector[2]
            for component in range(3)
        ]
    )


def local_field(padded, exch_kernel):
    forward = (padded[:, 2:, 1:-1, 1:-1], padded[:, 1:-1, 2:, 1:-1], padded[:, 1:-1, 1:-1, 2:])
    backward = (padded[:, :-2, 1:-1, 1:-1], padded[:, 1:-1, :-2, 1:-1], padded[:, 1:-1, 1:-1, :-2])
    summed = apply_kernel(exch_kernel[0], forward[0]) + apply_transposed(
        exch_kernel[0], backward[0]
    )
    for direction in (1, 2):
        summed = summed + apply_kernel(exch_kernel[direction], forward[direction])
        summed = summed + apply_transposed(exch_kernel[direction], backward[direction])
    return summed


def metropolis(spins, padded, exch_kernel, film_near, trial_move, uniform_draw, colour_mask):
    field_sum = local_field(padded, exch_kernel) + coupling_down * film_near
    proposal = normalized(spins + step_cone * trial_move)
    change = -jnp.sum((proposal - spins) * field_sum, axis=0) - anisotropy * (
        proposal[2] * proposal[2] - spins[2] * spins[2]
    )
    accept = jnp.exp(jnp.minimum(-inverse_temp * change, 0.0))
    weight = jax.nn.sigmoid((accept - uniform_draw) / softness)
    blended = normalized((1.0 - weight) * spins + weight * proposal)
    return jnp.where(colour_mask[None], blended, spins)


def sweep_kernel(step_ref, k_ref, s_ref, lo_ref, hi_ref, film_ref, valid_ref, trial_ref, unif_ref,
                 out_ref, olo_ref, ohi_ref):
    layers, rows_x, rows_y = s_ref.shape[1:]
    row = lax.broadcasted_iota(jnp.int32, (rows_x, rows_y), 0)
    col = lax.broadcasted_iota(jnp.int32, (rows_x, rows_y), 1)
    live = valid_ref[...] > 0.5
    sweep = step_ref[0]
    colour = step_ref[1]
    kk = [[[k_ref[d * 9 + a * 3 + b] for b in range(3)] for a in range(3)] for d in range(3)]
    for l in range(layers):
        s = [s_ref[c, l] for c in range(3)]
        below = [lo_ref[c, 0] if l == 0 else s_ref[c, l - 1] for c in range(3)]
        above = [hi_ref[c, 0] if l == layers - 1 else s_ref[c, l + 1] for c in range(3)]
        xp = [pltpu.roll(s[c], rows_x - 1, 0) for c in range(3)]
        xm = [pltpu.roll(s[c], 1, 0) for c in range(3)]
        yp = [pltpu.roll(s[c], rows_y - 1, 1) for c in range(3)]
        ym = [pltpu.roll(s[c], 1, 1) for c in range(3)]
        fwd = (above, xp, yp)
        bwd = (below, xm, ym)
        field = []
        for c in range(3):
            total = film_ref[c] * coupling_down
            for d in range(3):
                m = kk[d]
                total = total + (m[c][0] * fwd[d][0] + m[c][1] * fwd[d][1] + m[c][2] * fwd[d][2])
                total = total + (m[0][c] * bwd[d][0] + m[1][c] * bwd[d][1] + m[2][c] * bwd[d][2])
            field.append(total)
        raw = [s[c] + step_cone * trial_ref[sweep, c, l] for c in range(3)]
        norm = jnp.sqrt(raw[0] * raw[0] + raw[1] * raw[1] + raw[2] * raw[2])
        prop = [raw[c] / norm for c in range(3)]
        dot = (prop[0] - s[0]) * field[0] + (prop[1] - s[1]) * field[1] + (prop[2] - s[2]) * field[2]
        change = -dot - anisotropy * (prop[2] * prop[2] - s[2] * s[2])
        accept = jnp.exp(jnp.minimum(-inverse_temp * change, 0.0))
        weight = 1.0 / (1.0 + jnp.exp(-((accept - unif_ref[sweep, l]) / softness)))
        mix = [(1.0 - weight) * s[c] + weight * prop[c] for c in range(3)]
        mnorm = jnp.sqrt(mix[0] * mix[0] + mix[1] * mix[1] + mix[2] * mix[2])
        chosen = (((row + col + l) % 2) == colour) & live
        for c in range(3):
            new = jnp.where(chosen, mix[c] / mnorm, s[c])
            out_ref[c, l] = new
            if l == 0:
                olo_ref[c, 0] = new
            if l == layers - 1:
                ohi_ref[c, 0] = new


def half_sweep(spins, lo, hi, exch_flat, film_e, valid, trials, uniforms, sweep, colour):
    comps, layers, rows_x, rows_y = spins.shape
    vmem = pl.BlockSpec(memory_space=pltpu.VMEM)
    smem = pl.BlockSpec(memory_space=pltpu.SMEM)
    dt = spins.dtype
    face = jax.ShapeDtypeStruct((comps, 1, rows_x, rows_y), dt)
    out_shape = (jax.ShapeDtypeStruct(spins.shape, dt), face, face)
    sites = layers * rows_x * rows_y
    return pl.pallas_call(
        sweep_kernel,
        out_shape=out_shape,
        in_specs=[smem, smem] + [vmem] * 7,
        out_specs=tuple([vmem] * 3),
        cost_estimate=pl.CostEstimate(flops=200 * sites, transcendentals=4 * sites, bytes_accessed=4 * 14 * sites),
    )(jnp.array([sweep, colour], jnp.int32), exch_flat, spins, lo, hi, film_e, valid, trials, uniforms)


def shift_in(array, axis, from_lower):
    count = lax.axis_size(axis)
    up = [(i, i + 1) for i in range(count - 1)]
    return lax.ppermute(array, axis, up if from_lower else [(b, a) for a, b in up])


def extended(array, width, wide):
    rows, cols = array.shape[-2:]
    below = shift_in(array[..., rows - width :, :], GX, True)
    above = shift_in(array[..., :width, :], GX, False)
    array = jnp.concatenate([array, above, below], axis=-2)
    left = shift_in(jnp.swapaxes(array[..., cols - width :], -1, -2), GY, True)
    right = shift_in(jnp.swapaxes(array[..., :width], -1, -2), GY, False)
    gap = jnp.zeros(array.shape[:-1] + (wide - cols - 2 * width,), array.dtype)
    return jnp.concatenate(
        [array, jnp.swapaxes(right, -1, -2), gap, jnp.swapaxes(left, -1, -2)], axis=-1
    )


def cells_for_sites(patch, rows_x, rows_y, width, wide):
    inner = jnp.repeat(patch[:, 1:-1], K, axis=1)
    rows = jnp.concatenate(
        [inner, jnp.repeat(patch[:, -1:], width, axis=1), jnp.repeat(patch[:, :1], width, axis=1)], axis=1
    )
    inner = jnp.repeat(rows[:, :, 1:-1], K, axis=2)
    gap = jnp.zeros(rows.shape[:2] + (wide - rows_y - 2 * width,), rows.dtype)
    return jnp.concatenate(
        [inner, jnp.repeat(rows[:, :, -1:], width, axis=2), gap, jnp.repeat(rows[:, :, :1], width, axis=2)],
        axis=2,
    )


def cross_product(left, right):
    return jnp.stack(
        [
            left[1] * right[2] - left[2] * right[1],
            left[2] * right[0] - left[0] * right[2],
            left[0] * right[1] - left[1] * right[0],
        ]
    )


def film_rate(magnet, padded, film_anis, interface):
    laplace_sum = (
        padded[:, 2:, 1:-1]
        + padded[:, :-2, 1:-1]
        + padded[:, 1:-1, 2:]
        + padded[:, 1:-1, :-2]
        - 4.0 * magnet
    )
    field_sum = laplace_sum + coupling_up * interface
    field_sum = jnp.stack([field_sum[0], field_sum[1], field_sum[2] + film_anis * magnet[2]])
    precession = cross_product(magnet, field_sum)
    relaxation = cross_product(magnet, precession)
    return -(precession + damping * relaxation) / (1.0 + damping * damping)


def film_halo(magnet):
    return with_halo(magnet, ((REGION_GX, 1), (GY, 2)), 1)


def body(spins, uniforms, trials, exch_kernel, film_m, film_anis):
    layers_dev = spins.shape[1]
    rows_x = spins.shape[2]
    rows_y = spins.shape[3]
    piece_x = rows_x // K
    piece_y = rows_y // K
    gx_count = lax.axis_size(GX)
    gy_count = lax.axis_size(GY)
    tile_count = gx_count * gy_count
    region_pos = lax.axis_index("region")
    gx_pos = lax.axis_index(GX)
    gy_pos = lax.axis_index(GY)
    first_tile = (region_pos == 0) & (gx_pos == 0) & (gy_pos == 0)
    film_block = film_m[:, : piece_x * gx_count, : piece_y * gy_count]
    stack_spins, unif_all, trial_all = (spins, uniforms, trials)
    assert layers_dev % 2 == 0 and rows_x % 2 == 0 and rows_y % 2 == 0
    width = 2 * SWEEPS
    ext_x = rows_x + 2 * width
    wide = -(-(rows_y + 2 * width) // 128) * 128
    assert ext_x % 2 == 0 and wide % 2 == 0 and width <= K and width <= rows_x and width <= rows_y
    ring = jnp.pad(film_block, ((0, 0), (1, 1 + piece_x), (1, 1 + piece_y)))
    by_rows = jnp.stack(
        [ring[:, k : k + piece_x * gx_count].reshape(3, gx_count, piece_x, -1)[:, :, 0] for k in range(piece_x + 2)]
    )
    by_cols = jnp.stack(
        [by_rows[..., q : q + piece_y * gy_count].reshape(*by_rows.shape[:3], gy_count, piece_y)[..., 0] for q in range(piece_y + 2)]
    )
    pieces = by_cols.transpose(3, 4, 2, 1, 0).reshape(tile_count, 3, piece_x + 2, piece_y + 2)
    pieces = jnp.where(first_tile, pieces, 0.0)
    placed = summed_rows(pieces, (("gx_0", "gx_1", "gy_0"), "gy_1"), 0)[0]
    own_patch = picked(placed, "region", 0)
    film_e = cells_for_sites(own_patch, rows_x, rows_y, width, wide)
    exch_flat = exch_kernel.reshape(-1)
    channels = jnp.concatenate(
        [stack_spins, trial_all.reshape(-1, layers_dev, rows_x, rows_y), unif_all], axis=0
    )
    channels = extended(channels, width, wide)
    spins_e = channels[:3]
    trials_e = channels[3 : 3 + 3 * SWEEPS].reshape(SWEEPS, 3, layers_dev, ext_x, wide)
    unif_e = channels[3 + 3 * SWEEPS :]
    local_x = jnp.arange(ext_x, dtype=jnp.int32)
    local_x = jnp.where(local_x < rows_x + width, local_x, local_x - ext_x)
    local_y = jnp.arange(wide, dtype=jnp.int32)
    real_y = (local_y < rows_y + width) | (local_y >= wide - width)
    local_y = jnp.where(local_y < rows_y + width, local_y, local_y - wide)
    global_x = gx_pos * rows_x + local_x
    global_y = gy_pos * rows_y + local_y
    valid_x = (global_x >= 0) & (global_x < rows_x * gx_count)
    valid_y = real_y & (global_y >= 0) & (global_y < rows_y * gy_count)
    valid = (valid_x[:, None] & valid_y[None, :]).astype(jnp.float32)
    lo = spins_e[:, :1]
    hi = spins_e[:, -1:]
    for sweep_index in range(SWEEPS):
        for colour in (0, 1):
            below = shift_in(hi, "region", True)
            above = shift_in(lo, "region", False)
            spins_e, lo, hi = half_sweep(
                spins_e, below, above, exch_flat, film_e, valid, trials_e, unif_e, sweep_index, colour
            )
    stack_spins = spins_e[:, :, :rows_x, :rows_y]
    averages = stack_spins[:, 0].reshape(3, piece_x, K, piece_y, K).mean(axis=(2, 4))
    gathered = whole_of(averages[None], (("gx_0", "gx_1", "gy_0"), "gy_1"), 0)
    assembled = (
        gathered.reshape(gx_count, gy_count, 3, piece_x, piece_y)
        .transpose(2, 0, 3, 1, 4)
        .reshape(3, gx_count * piece_x, gy_count * piece_y)
    )
    padded_block = jnp.pad(
        assembled,
        (
            (0, 0),
            (0, film_m.shape[1] - assembled.shape[1]),
            (0, film_m.shape[2] - assembled.shape[2]),
        ),
    )
    interface = jnp.where(first_tile, padded_block, 0.0)
    rate_start = film_rate(film_m, film_halo(film_m), film_anis, interface)
    predicted = film_m + time_step * rate_start
    rate_trial = film_rate(predicted, film_halo(predicted), film_anis, interface)
    corrected = film_m + 0.5 * time_step * (rate_start + rate_trial)
    return (stack_spins, normalized(corrected))


def solution(mesh):
    finer = Mesh(
        mesh.devices.reshape(mesh.shape["region"], 8, 2, 4, 2),
        ("region", "gx_0", "gx_1", "gy_0", "gy_1"),
    )
    in_specs = (
        P(None, "region", GX, GY),
        P(None, "region", GX, GY),
        P(None, None, "region", GX, GY),
        P(),
        P(None, REGION_GX, GY),
        P(REGION_GX, GY),
    )
    out_specs = (P(None, "region", GX, GY), P(None, REGION_GX, GY))
    return jax.shard_map(body, mesh=finer, in_specs=in_specs, out_specs=out_specs, check_vma=False)
```

```python
import functools

import jax
import jax.numpy as jnp
from jax import lax
from jax.sharding import Mesh
from jax.sharding import PartitionSpec as P
from jax.experimental import pallas as pl
from jax.experimental.pallas import tpu as pltpu

K = 8
SWEEPS = 2
REGION_GX = ("region", "gx_0", "gx_1")
GY = ("gy_0", "gy_1")
GX = ("gx_0", "gx_1")


coupling_down = 1.0
anisotropy = 0.5
inverse_temp = 2.0
softness = 0.05
step_cone = 0.4
coupling_up = 2.0
damping = 0.1
time_step = 0.05


def with_halo(array, sides, width):
    edges = {}
    for axis, dim in sides:
        count, length = (lax.axis_size(axis), array.shape[dim])
        up = [(i, (i + 1) % count) for i in range(count - 1)]
        last = lax.slice_in_dim(array, length - width, length, axis=dim)
        leading = lax.slice_in_dim(array, 0, width, axis=dim)
        edges[dim] = (
            lax.ppermute(last, axis, up),
            lax.ppermute(leading, axis, [(b, a) for a, b in up]),
        )
    done = []
    for _, dim in sides:
        low, high = edges[dim]
        around = [(width, width) if d in done else (0, 0) for d in range(array.ndim)]
        array = jnp.concatenate([jnp.pad(low, around), array, jnp.pad(high, around)], axis=dim)
        done.append(dim)
    return array


def split_up(array, dim, count):
    shape = array.shape
    parts = array.reshape(*shape[:dim], count, shape[dim] // count, *shape[dim + 1 :])
    return jnp.moveaxis(parts, dim, 0)


def summed_on_arrival(array, axis, dim):
    parts = split_up(array, dim, lax.axis_size(axis))
    arrived = lax.all_to_all(parts, axis, split_axis=0, concat_axis=0, tiled=True)
    return arrived.sum(axis=0)


def summed_rows(array, axes, dim):
    far, near = axes
    own = summed_on_arrival(split_up(array, dim, lax.axis_size(far)), near, dim + 1)
    return jnp.sum(lax.all_to_all(own, far, 0, 0, tiled=True), axis=0)


def picked(array, axis, root):
    return lax.dynamic_index_in_dim(lax.all_gather(array, axis), root, 0, keepdims=False)


def copy_for_each(array, axis):
    count = lax.axis_size(axis)
    return lax.all_to_all(
        jnp.broadcast_to(array[None], (count, *array.shape)), axis, 0, 0, tiled=True
    )


def laid_out(parts, dim):
    shape = list(parts.shape[1:])
    shape[dim] *= parts.shape[0]
    return jnp.moveaxis(parts, 0, dim).reshape(shape)


def whole_of(array, axes, dim):
    far, near = axes
    parts = copy_for_each(copy_for_each(array, far), near)
    return laid_out(parts.swapaxes(0, 1).reshape(-1, *array.shape), dim)


def normalized(vector):
    return vector / jnp.sqrt(jnp.sum(vector * vector, axis=0, keepdims=True))


def apply_kernel(matrix, vector):
    return jnp.stack(
        [
            matrix[component, 0] * vector[0]
            + matrix[component, 1] * vector[1]
            + matrix[component, 2] * vector[2]
            for component in range(3)
        ]
    )


def apply_transposed(matrix, vector):
    return jnp.stack(
        [
            matrix[0, component] * vector[0]
            + matrix[1, component] * vector[1]
            + matrix[2, component] * vector[2]
            for component in range(3)
        ]
    )


def local_field(padded, exch_kernel):
    forward = (padded[:, 2:, 1:-1, 1:-1], padded[:, 1:-1, 2:, 1:-1], padded[:, 1:-1, 1:-1, 2:])
    backward = (padded[:, :-2, 1:-1, 1:-1], padded[:, 1:-1, :-2, 1:-1], padded[:, 1:-1, 1:-1, :-2])
    summed = apply_kernel(exch_kernel[0], forward[0]) + apply_transposed(
        exch_kernel[0], backward[0]
    )
    for direction in (1, 2):
        summed = summed + apply_kernel(exch_kernel[direction], forward[direction])
        summed = summed + apply_transposed(exch_kernel[direction], backward[direction])
    return summed


def metropolis(spins, padded, exch_kernel, film_near, trial_move, uniform_draw, colour_mask):
    field_sum = local_field(padded, exch_kernel) + coupling_down * film_near
    proposal = normalized(spins + step_cone * trial_move)
    change = -jnp.sum((proposal - spins) * field_sum, axis=0) - anisotropy * (
        proposal[2] * proposal[2] - spins[2] * spins[2]
    )
    accept = jnp.exp(jnp.minimum(-inverse_temp * change, 0.0))
    weight = jax.nn.sigmoid((accept - uniform_draw) / softness)
    blended = normalized((1.0 - weight) * spins + weight * proposal)
    return jnp.where(colour_mask[None], blended, spins)


def sweep_kernel(step_ref, k_ref, s_ref, lo_ref, hi_ref, film_ref, valid_ref, trial_ref, unif_ref,
                 out_ref, olo_ref, ohi_ref):
    layers, rows_x, rows_y = s_ref.shape[1:]
    row = lax.broadcasted_iota(jnp.int32, (rows_x, rows_y), 0)
    col = lax.broadcasted_iota(jnp.int32, (rows_x, rows_y), 1)
    live = valid_ref[...] > 0.5
    sweep = step_ref[0]
    colour = step_ref[1]
    kk = [[[k_ref[d * 9 + a * 3 + b] for b in range(3)] for a in range(3)] for d in range(3)]
    for l in range(layers):
        s = [s_ref[c, l] for c in range(3)]
        below = [lo_ref[c, 0] if l == 0 else s_ref[c, l - 1] for c in range(3)]
        above = [hi_ref[c, 0] if l == layers - 1 else s_ref[c, l + 1] for c in range(3)]
        xp = [pltpu.roll(s[c], rows_x - 1, 0) for c in range(3)]
        xm = [pltpu.roll(s[c], 1, 0) for c in range(3)]
        yp = [pltpu.roll(s[c], rows_y - 1, 1) for c in range(3)]
        ym = [pltpu.roll(s[c], 1, 1) for c in range(3)]
        fwd = (above, xp, yp)
        bwd = (below, xm, ym)
        field = []
        for c in range(3):
            total = film_ref[c] * coupling_down
            for d in range(3):
                m = kk[d]
                total = total + (m[c][0] * fwd[d][0] + m[c][1] * fwd[d][1] + m[c][2] * fwd[d][2])
                total = total + (m[0][c] * bwd[d][0] + m[1][c] * bwd[d][1] + m[2][c] * bwd[d][2])
            field.append(total)
        raw = [s[c] + step_cone * trial_ref[sweep, c, l] for c in range(3)]
        norm = jnp.sqrt(raw[0] * raw[0] + raw[1] * raw[1] + raw[2] * raw[2])
        prop = [raw[c] / norm for c in range(3)]
        dot = (prop[0] - s[0]) * field[0] + (prop[1] - s[1]) * field[1] + (prop[2] - s[2]) * field[2]
        change = -dot - anisotropy * (prop[2] * prop[2] - s[2] * s[2])
        accept = jnp.exp(jnp.minimum(-inverse_temp * change, 0.0))
        weight = 1.0 / (1.0 + jnp.exp(-((accept - unif_ref[sweep, l]) / softness)))
        mix = [(1.0 - weight) * s[c] + weight * prop[c] for c in range(3)]
        mnorm = jnp.sqrt(mix[0] * mix[0] + mix[1] * mix[1] + mix[2] * mix[2])
        chosen = (((row + col + l) % 2) == colour) & live
        for c in range(3):
            new = jnp.where(chosen, mix[c] / mnorm, s[c])
            out_ref[c, l] = new
            if l == 0:
                olo_ref[c, 0] = new
            if l == layers - 1:
                ohi_ref[c, 0] = new


def half_sweep(spins, lo, hi, exch_flat, film_e, valid, trials, uniforms, sweep, colour):
    comps, layers, rows_x, rows_y = spins.shape
    vmem = pl.BlockSpec(memory_space=pltpu.VMEM)
    smem = pl.BlockSpec(memory_space=pltpu.SMEM)
    dt = spins.dtype
    face = jax.ShapeDtypeStruct((comps, 1, rows_x, rows_y), dt)
    out_shape = (jax.ShapeDtypeStruct(spins.shape, dt), face, face)
    sites = layers * rows_x * rows_y
    return pl.pallas_call(
        sweep_kernel,
        out_shape=out_shape,
        in_specs=[smem, smem] + [vmem] * 7,
        out_specs=tuple([vmem] * 3),
        cost_estimate=pl.CostEstimate(flops=200 * sites, transcendentals=4 * sites, bytes_accessed=4 * 14 * sites),
    )(jnp.array([sweep, colour], jnp.int32), exch_flat, spins, lo, hi, film_e, valid, trials, uniforms)


def shift_in(array, axis, from_lower):
    count = lax.axis_size(axis)
    up = [(i, i + 1) for i in range(count - 1)]
    return lax.ppermute(array, axis, up if from_lower else [(b, a) for a, b in up])


def extended(array, width, wide):
    rows, cols = array.shape[-2:]
    below = shift_in(array[..., rows - width :, :], GX, True)
    above = shift_in(array[..., :width, :], GX, False)
    array = jnp.concatenate([array, above, below], axis=-2)
    left = shift_in(jnp.swapaxes(array[..., cols - width :], -1, -2), GY, True)
    right = shift_in(jnp.swapaxes(array[..., :width], -1, -2), GY, False)
    gap = jnp.zeros(array.shape[:-1] + (wide - cols - 2 * width,), array.dtype)
    return jnp.concatenate(
        [array, jnp.swapaxes(right, -1, -2), gap, jnp.swapaxes(left, -1, -2)], axis=-1
    )


def cells_for_sites(patch, rows_x, rows_y, width, wide):
    inner = jnp.repeat(patch[:, 1:-1], K, axis=1)
    rows = jnp.concatenate(
        [inner, jnp.repeat(patch[:, -1:], width, axis=1), jnp.repeat(patch[:, :1], width, axis=1)], axis=1
    )
    inner = jnp.repeat(rows[:, :, 1:-1], K, axis=2)
    gap = jnp.zeros(rows.shape[:2] + (wide - rows_y - 2 * width,), rows.dtype)
    return jnp.concatenate(
        [inner, jnp.repeat(rows[:, :, -1:], width, axis=2), gap, jnp.repeat(rows[:, :, :1], width, axis=2)],
        axis=2,
    )


def cross_product(left, right):
    return jnp.stack(
        [
            left[1] * right[2] - left[2] * right[1],
            left[2] * right[0] - left[0] * right[2],
            left[0] * right[1] - left[1] * right[0],
        ]
    )


def film_rate(magnet, padded, film_anis, interface):
    laplace_sum = (
        padded[:, 2:, 1:-1]
        + padded[:, :-2, 1:-1]
        + padded[:, 1:-1, 2:]
        + padded[:, 1:-1, :-2]
        - 4.0 * magnet
    )
    field_sum = laplace_sum + coupling_up * interface
    field_sum = jnp.stack([field_sum[0], field_sum[1], field_sum[2] + film_anis * magnet[2]])
    precession = cross_product(magnet, field_sum)
    relaxation = cross_product(magnet, precession)
    return -(precession + damping * relaxation) / (1.0 + damping * damping)


def film_halo(magnet):
    return with_halo(magnet, ((REGION_GX, 1), (GY, 2)), 1)


def body(spins, uniforms, trials, exch_kernel, film_m, film_anis):
    layers_dev = spins.shape[1]
    rows_x = spins.shape[2]
    rows_y = spins.shape[3]
    piece_x = rows_x // K
    piece_y = rows_y // K
    gx_count = lax.axis_size(GX)
    gy_count = lax.axis_size(GY)
    tile_count = gx_count * gy_count
    region_pos = lax.axis_index("region")
    gx_pos = lax.axis_index(GX)
    gy_pos = lax.axis_index(GY)
    first_tile = (region_pos == 0) & (gx_pos == 0) & (gy_pos == 0)
    film_block = film_m[:, : piece_x * gx_count, : piece_y * gy_count]
    stack_spins, unif_all, trial_all = (spins, uniforms, trials)
    assert layers_dev % 2 == 0 and rows_x % 2 == 0 and rows_y % 2 == 0
    width = 2 * SWEEPS
    ext_x = rows_x + 2 * width
    wide = -(-(rows_y + 2 * width) // 128) * 128
    assert ext_x % 2 == 0 and wide % 2 == 0 and width <= K and width <= rows_x and width <= rows_y
    tiles = film_block.reshape(3, gx_count, piece_x, gy_count, piece_y).transpose(1, 3, 0, 2, 4)
    zero_row = jnp.zeros_like(tiles[:1, :, :, :1])
    tiles = jnp.concatenate(
        [
            jnp.concatenate([zero_row, tiles[:-1, :, :, -1:]], axis=0),
            tiles,
            jnp.concatenate([tiles[1:, :, :, :1], zero_row], axis=0),
        ],
        axis=3,
    )
    zero_col = jnp.zeros_like(tiles[:, :1, :, :, :1])
    tiles = jnp.concatenate(
        [
            jnp.concatenate([zero_col, tiles[:, :-1, :, :, -1:]], axis=1),
            tiles,
            jnp.concatenate([tiles[:, 1:, :, :, :1], zero_col], axis=1),
        ],
        axis=4,
    )
    pieces = tiles.reshape(tile_count, 3, piece_x + 2, piece_y + 2)
    pieces = jnp.where(first_tile, pieces, 0.0)
    placed = summed_rows(pieces, (("gx_0", "gx_1", "gy_0"), "gy_1"), 0)[0]
    own_patch = picked(placed, "region", 0)
    film_e = cells_for_sites(own_patch, rows_x, rows_y, width, wide)
    exch_flat = exch_kernel.reshape(-1)
    channels = jnp.concatenate(
        [stack_spins, trial_all.reshape(-1, layers_dev, rows_x, rows_y), unif_all], axis=0
    )
    channels = extended(channels, width, wide)
    spins_e = channels[:3]
    trials_e = channels[3 : 3 + 3 * SWEEPS].reshape(SWEEPS, 3, layers_dev, ext_x, wide)
    unif_e = channels[3 + 3 * SWEEPS :]
    local_x = jnp.arange(ext_x, dtype=jnp.int32)
    local_x = jnp.where(local_x < rows_x + width, local_x, local_x - ext_x)
    local_y = jnp.arange(wide, dtype=jnp.int32)
    real_y = (local_y < rows_y + width) | (local_y >= wide - width)
    local_y = jnp.where(local_y < rows_y + width, local_y, local_y - wide)
    global_x = gx_pos * rows_x + local_x
    global_y = gy_pos * rows_y + local_y
    valid_x = (global_x >= 0) & (global_x < rows_x * gx_count)
    valid_y = real_y & (global_y >= 0) & (global_y < rows_y * gy_count)
    valid = (valid_x[:, None] & valid_y[None, :]).astype(jnp.float32)
    lo = spins_e[:, :1]
    hi = spins_e[:, -1:]
    for sweep_index in range(SWEEPS):
        for colour in (0, 1):
            below = shift_in(hi, "region", True)
            above = shift_in(lo, "region", False)
            spins_e, lo, hi = half_sweep(
                spins_e, below, above, exch_flat, film_e, valid, trials_e, unif_e, sweep_index, colour
            )
    stack_spins = spins_e[:, :, :rows_x, :rows_y]
    averages = stack_spins[:, 0].reshape(3, piece_x, K, piece_y, K).mean(axis=(2, 4))
    gathered = whole_of(averages[None], (("gx_0", "gx_1", "gy_0"), "gy_1"), 0)
    assembled = (
        gathered.reshape(gx_count, gy_count, 3, piece_x, piece_y)
        .transpose(2, 0, 3, 1, 4)
        .reshape(3, gx_count * piece_x, gy_count * piece_y)
    )
    padded_block = jnp.pad(
        assembled,
        (
            (0, 0),
            (0, film_m.shape[1] - assembled.shape[1]),
            (0, film_m.shape[2] - assembled.shape[2]),
        ),
    )
    interface = jnp.where(first_tile, padded_block, 0.0)
    rate_start = film_rate(film_m, film_halo(film_m), film_anis, interface)
    predicted = film_m + time_step * rate_start
    rate_trial = film_rate(predicted, film_halo(predicted), film_anis, interface)
    corrected = film_m + 0.5 * time_step * (rate_start + rate_trial)
    return (stack_spins, normalized(corrected))


def solution(mesh):
    finer = Mesh(
        mesh.devices.reshape(mesh.shape["region"], 8, 2, 4, 2),
        ("region", "gx_0", "gx_1", "gy_0", "gy_1"),
    )
    in_specs = (
        P(None, "region", GX, GY),
        P(None, "region", GX, GY),
        P(None, None, "region", GX, GY),
        P(),
        P(None, REGION_GX, GY),
        P(REGION_GX, GY),
    )
    out_specs = (P(None, "region", GX, GY), P(None, REGION_GX, GY))
    return jax.shard_map(body, mesh=finer, in_specs=in_specs, out_specs=out_specs, check_vma=False)
```

```python
import functools

import jax
import jax.numpy as jnp
from jax import lax
from jax.sharding import Mesh
from jax.sharding import PartitionSpec as P
from jax.experimental import pallas as pl
from jax.experimental.pallas import tpu as pltpu

K = 8
SWEEPS = 2
REGION_GX = ("region", "gx_0", "gx_1")
GY = ("gy_0", "gy_1")
GX = ("gx_0", "gx_1")


coupling_down = 1.0
anisotropy = 0.5
inverse_temp = 2.0
softness = 0.05
step_cone = 0.4
coupling_up = 2.0
damping = 0.1
time_step = 0.05


def with_halo(array, sides, width):
    edges = {}
    for axis, dim in sides:
        count, length = (lax.axis_size(axis), array.shape[dim])
        up = [(i, (i + 1) % count) for i in range(count - 1)]
        last = lax.slice_in_dim(array, length - width, length, axis=dim)
        leading = lax.slice_in_dim(array, 0, width, axis=dim)
        edges[dim] = (
            lax.ppermute(last, axis, up),
            lax.ppermute(leading, axis, [(b, a) for a, b in up]),
        )
    done = []
    for _, dim in sides:
        low, high = edges[dim]
        around = [(width, width) if d in done else (0, 0) for d in range(array.ndim)]
        array = jnp.concatenate([jnp.pad(low, around), array, jnp.pad(high, around)], axis=dim)
        done.append(dim)
    return array


def split_up(array, dim, count):
    shape = array.shape
    parts = array.reshape(*shape[:dim], count, shape[dim] // count, *shape[dim + 1 :])
    return jnp.moveaxis(parts, dim, 0)


def summed_on_arrival(array, axis, dim):
    parts = split_up(array, dim, lax.axis_size(axis))
    arrived = lax.all_to_all(parts, axis, split_axis=0, concat_axis=0, tiled=True)
    return arrived.sum(axis=0)


def summed_rows(array, axes, dim):
    far, near = axes
    own = summed_on_arrival(split_up(array, dim, lax.axis_size(far)), near, dim + 1)
    return jnp.sum(lax.all_to_all(own, far, 0, 0, tiled=True), axis=0)


def picked(array, axis, root):
    return lax.dynamic_index_in_dim(lax.all_gather(array, axis), root, 0, keepdims=False)


def copy_for_each(array, axis):
    count = lax.axis_size(axis)
    return lax.all_to_all(
        jnp.broadcast_to(array[None], (count, *array.shape)), axis, 0, 0, tiled=True
    )


def laid_out(parts, dim):
    shape = list(parts.shape[1:])
    shape[dim] *= parts.shape[0]
    return jnp.moveaxis(parts, 0, dim).reshape(shape)


def whole_of(array, axes, dim):
    far, near = axes
    parts = copy_for_each(copy_for_each(array, far), near)
    return laid_out(parts.swapaxes(0, 1).reshape(-1, *array.shape), dim)


def normalized(vector):
    return vector / jnp.sqrt(jnp.sum(vector * vector, axis=0, keepdims=True))


def apply_kernel(matrix, vector):
    return jnp.stack(
        [
            matrix[component, 0] * vector[0]
            + matrix[component, 1] * vector[1]
            + matrix[component, 2] * vector[2]
            for component in range(3)
        ]
    )


def apply_transposed(matrix, vector):
    return jnp.stack(
        [
            matrix[0, component] * vector[0]
            + matrix[1, component] * vector[1]
            + matrix[2, component] * vector[2]
            for component in range(3)
        ]
    )


def local_field(padded, exch_kernel):
    forward = (padded[:, 2:, 1:-1, 1:-1], padded[:, 1:-1, 2:, 1:-1], padded[:, 1:-1, 1:-1, 2:])
    backward = (padded[:, :-2, 1:-1, 1:-1], padded[:, 1:-1, :-2, 1:-1], padded[:, 1:-1, 1:-1, :-2])
    summed = apply_kernel(exch_kernel[0], forward[0]) + apply_transposed(
        exch_kernel[0], backward[0]
    )
    for direction in (1, 2):
        summed = summed + apply_kernel(exch_kernel[direction], forward[direction])
        summed = summed + apply_transposed(exch_kernel[direction], backward[direction])
    return summed


def metropolis(spins, padded, exch_kernel, film_near, trial_move, uniform_draw, colour_mask):
    field_sum = local_field(padded, exch_kernel) + coupling_down * film_near
    proposal = normalized(spins + step_cone * trial_move)
    change = -jnp.sum((proposal - spins) * field_sum, axis=0) - anisotropy * (
        proposal[2] * proposal[2] - spins[2] * spins[2]
    )
    accept = jnp.exp(jnp.minimum(-inverse_temp * change, 0.0))
    weight = jax.nn.sigmoid((accept - uniform_draw) / softness)
    blended = normalized((1.0 - weight) * spins + weight * proposal)
    return jnp.where(colour_mask[None], blended, spins)


def sweep_kernel(step_ref, k_ref, s_ref, lo_ref, hi_ref, film_ref, valid_ref, trial_ref, unif_ref,
                 out_ref, olo_ref, ohi_ref):
    layers, rows_x, rows_y = s_ref.shape[1:]
    row = lax.broadcasted_iota(jnp.int32, (rows_x, rows_y), 0)
    col = lax.broadcasted_iota(jnp.int32, (rows_x, rows_y), 1)
    live = valid_ref[...] > 0.5
    sweep = step_ref[0]
    colour = step_ref[1]
    kk = [[[k_ref[d * 9 + a * 3 + b] for b in range(3)] for a in range(3)] for d in range(3)]
    for l in range(layers):
        s = [s_ref[c, l] for c in range(3)]
        below = [lo_ref[c, 0] if l == 0 else s_ref[c, l - 1] for c in range(3)]
        above = [hi_ref[c, 0] if l == layers - 1 else s_ref[c, l + 1] for c in range(3)]
        xp = [pltpu.roll(s[c], rows_x - 1, 0) for c in range(3)]
        xm = [pltpu.roll(s[c], 1, 0) for c in range(3)]
        yp = [pltpu.roll(s[c], rows_y - 1, 1) for c in range(3)]
        ym = [pltpu.roll(s[c], 1, 1) for c in range(3)]
        fwd = (above, xp, yp)
        bwd = (below, xm, ym)
        field = []
        for c in range(3):
            total = film_ref[c] * coupling_down
            for d in range(3):
                m = kk[d]
                total = total + (m[c][0] * fwd[d][0] + m[c][1] * fwd[d][1] + m[c][2] * fwd[d][2])
                total = total + (m[0][c] * bwd[d][0] + m[1][c] * bwd[d][1] + m[2][c] * bwd[d][2])
            field.append(total)
        raw = [s[c] + step_cone * trial_ref[sweep, c, l] for c in range(3)]
        norm = jnp.sqrt(raw[0] * raw[0] + raw[1] * raw[1] + raw[2] * raw[2])
        prop = [raw[c] / norm for c in range(3)]
        dot = (prop[0] - s[0]) * field[0] + (prop[1] - s[1]) * field[1] + (prop[2] - s[2]) * field[2]
        change = -dot - anisotropy * (prop[2] * prop[2] - s[2] * s[2])
        accept = jnp.exp(jnp.minimum(-inverse_temp * change, 0.0))
        weight = 1.0 / (1.0 + jnp.exp(-((accept - unif_ref[sweep, l]) / softness)))
        mix = [(1.0 - weight) * s[c] + weight * prop[c] for c in range(3)]
        mnorm = jnp.sqrt(mix[0] * mix[0] + mix[1] * mix[1] + mix[2] * mix[2])
        chosen = (((row + col + l) % 2) == colour) & live
        for c in range(3):
            new = jnp.where(chosen, mix[c] / mnorm, s[c])
            out_ref[c, l] = new
            if l == 0:
                olo_ref[c, 0] = new
            if l == layers - 1:
                ohi_ref[c, 0] = new


def half_sweep(spins, lo, hi, exch_flat, film_e, valid, trials, uniforms, sweep, colour):
    comps, layers, rows_x, rows_y = spins.shape
    vmem = pl.BlockSpec(memory_space=pltpu.VMEM)
    smem = pl.BlockSpec(memory_space=pltpu.SMEM)
    dt = spins.dtype
    face = jax.ShapeDtypeStruct((comps, 1, rows_x, rows_y), dt)
    out_shape = (jax.ShapeDtypeStruct(spins.shape, dt), face, face)
    sites = layers * rows_x * rows_y
    return pl.pallas_call(
        sweep_kernel,
        out_shape=out_shape,
        in_specs=[smem, smem] + [vmem] * 7,
        out_specs=tuple([vmem] * 3),
        cost_estimate=pl.CostEstimate(flops=200 * sites, transcendentals=4 * sites, bytes_accessed=4 * 14 * sites),
    )(jnp.array([sweep, colour], jnp.int32), exch_flat, spins, lo, hi, film_e, valid, trials, uniforms)


def shift_in(array, axis, from_lower):
    count = lax.axis_size(axis)
    up = [(i, i + 1) for i in range(count - 1)]
    return lax.ppermute(array, axis, up if from_lower else [(b, a) for a, b in up])


def packed(*arrays):
    return jnp.concatenate([array.reshape(-1) for array in arrays])


def unpacked(flat, *likes):
    out, at = [], 0
    for like in likes:
        out.append(flat[at : at + like.size].reshape(like.shape))
        at += like.size
    return out


def extended(array, film, width, film_width, wide):
    rows, cols = array.shape[-2:]
    gx_pos = lax.axis_index(GX)
    last = lax.axis_size(GX) - 1
    s_low, f_low = array[..., rows - width :, :], film[:, -film_width:, :]
    s_high, f_high = array[..., :width, :], film[:, :film_width, :]
    below = unpacked(shift_in(packed(s_low, f_low), REGION_GX, True), s_low, f_low)
    above = unpacked(shift_in(packed(s_high, f_high), REGION_GX, False), s_high, f_high)
    array = jnp.concatenate(
        [array, jnp.where(gx_pos == last, 0.0, above[0]), jnp.where(gx_pos == 0, 0.0, below[0])], axis=-2
    )
    film = jnp.concatenate([below[1], film, above[1]], axis=1)
    s_low = jnp.swapaxes(array[..., cols - width :], -1, -2)
    f_low = jnp.swapaxes(film[:, :, -film_width:], -1, -2)
    s_high = jnp.swapaxes(array[..., :width], -1, -2)
    f_high = jnp.swapaxes(film[:, :, :film_width], -1, -2)
    left = unpacked(shift_in(packed(s_low, f_low), GY, True), s_low, f_low)
    right = unpacked(shift_in(packed(s_high, f_high), GY, False), s_high, f_high)
    gap = jnp.zeros(array.shape[:-1] + (wide - cols - 2 * width,), array.dtype)
    array = jnp.concatenate(
        [array, jnp.swapaxes(right[0], -1, -2), gap, jnp.swapaxes(left[0], -1, -2)], axis=-1
    )
    film = jnp.concatenate(
        [jnp.swapaxes(left[1], -1, -2), film, jnp.swapaxes(right[1], -1, -2)], axis=-1
    )
    return array, film


def cells_for_sites(patch, rows_x, rows_y, width, wide):
    inner = jnp.repeat(patch[:, 1:-1], K, axis=1)
    rows = jnp.concatenate(
        [inner, jnp.repeat(patch[:, -1:], width, axis=1), jnp.repeat(patch[:, :1], width, axis=1)], axis=1
    )
    inner = jnp.repeat(rows[:, :, 1:-1], K, axis=2)
    gap = jnp.zeros(rows.shape[:2] + (wide - rows_y - 2 * width,), rows.dtype)
    return jnp.concatenate(
        [inner, jnp.repeat(rows[:, :, -1:], width, axis=2), gap, jnp.repeat(rows[:, :, :1], width, axis=2)],
        axis=2,
    )


def cross_product(left, right):
    return jnp.stack(
        [
            left[1] * right[2] - left[2] * right[1],
            left[2] * right[0] - left[0] * right[2],
            left[0] * right[1] - left[1] * right[0],
        ]
    )


def film_rate(magnet, padded, film_anis, interface):
    laplace_sum = (
        padded[:, 2:, 1:-1]
        + padded[:, :-2, 1:-1]
        + padded[:, 1:-1, 2:]
        + padded[:, 1:-1, :-2]
        - 4.0 * magnet
    )
    field_sum = laplace_sum + coupling_up * interface
    field_sum = jnp.stack([field_sum[0], field_sum[1], field_sum[2] + film_anis * magnet[2]])
    precession = cross_product(magnet, field_sum)
    relaxation = cross_product(magnet, precession)
    return -(precession + damping * relaxation) / (1.0 + damping * damping)


def film_halo(magnet):
    return with_halo(magnet, ((REGION_GX, 1), (GY, 2)), 1)


def body(spins, uniforms, trials, exch_kernel, film_m, film_anis):
    layers_dev = spins.shape[1]
    rows_x = spins.shape[2]
    rows_y = spins.shape[3]
    piece_x = rows_x // K
    piece_y = rows_y // K
    gx_count = lax.axis_size(GX)
    gy_count = lax.axis_size(GY)
    tile_count = gx_count * gy_count
    region_pos = lax.axis_index("region")
    gx_pos = lax.axis_index(GX)
    gy_pos = lax.axis_index(GY)
    first_tile = (region_pos == 0) & (gx_pos == 0) & (gy_pos == 0)
    film_block = film_m[:, : piece_x * gx_count, : piece_y * gy_count]
    stack_spins, unif_all, trial_all = (spins, uniforms, trials)
    assert layers_dev % 2 == 0 and rows_x % 2 == 0 and rows_y % 2 == 0
    width = 2 * SWEEPS
    ext_x = rows_x + 2 * width
    wide = -(-(rows_y + 2 * width) // 128) * 128
    assert ext_x % 2 == 0 and wide % 2 == 0 and width <= K and width <= rows_x and width <= rows_y
    tiles = film_block.reshape(3, gx_count, piece_x, gy_count, piece_y).transpose(1, 3, 0, 2, 4)
    zero_row = jnp.zeros_like(tiles[:1, :, :, :1])
    tiles = jnp.concatenate(
        [
            jnp.concatenate([zero_row, tiles[:-1, :, :, -1:]], axis=0),
            tiles,
            jnp.concatenate([tiles[1:, :, :, :1], zero_row], axis=0),
        ],
        axis=3,
    )
    zero_col = jnp.zeros_like(tiles[:, :1, :, :, :1])
    tiles = jnp.concatenate(
        [
            jnp.concatenate([zero_col, tiles[:, :-1, :, :, -1:]], axis=1),
            tiles,
            jnp.concatenate([tiles[:, 1:, :, :, :1], zero_col], axis=1),
        ],
        axis=4,
    )
    pieces = tiles.reshape(tile_count, 3, piece_x + 2, piece_y + 2)
    pieces = jnp.where(first_tile, pieces, 0.0)
    placed = summed_rows(pieces, (("gx_0", "gx_1", "gy_0"), "gy_1"), 0)[0]
    own_patch = picked(placed, "region", 0)
    film_e = cells_for_sites(own_patch, rows_x, rows_y, width, wide)
    exch_flat = exch_kernel.reshape(-1)
    channels = jnp.concatenate(
        [stack_spins, trial_all.reshape(-1, layers_dev, rows_x, rows_y), unif_all], axis=0
    )
    film_width = 2
    film_all = jnp.concatenate([film_m, film_anis[None]], axis=0)
    channels, film_e4 = extended(channels, film_all, width, film_width, wide)
    spins_e = channels[:3]
    trials_e = channels[3 : 3 + 3 * SWEEPS].reshape(SWEEPS, 3, layers_dev, ext_x, wide)
    unif_e = channels[3 + 3 * SWEEPS :]
    local_x = jnp.arange(ext_x, dtype=jnp.int32)
    local_x = jnp.where(local_x < rows_x + width, local_x, local_x - ext_x)
    local_y = jnp.arange(wide, dtype=jnp.int32)
    real_y = (local_y < rows_y + width) | (local_y >= wide - width)
    local_y = jnp.where(local_y < rows_y + width, local_y, local_y - wide)
    global_x = gx_pos * rows_x + local_x
    global_y = gy_pos * rows_y + local_y
    valid_x = (global_x >= 0) & (global_x < rows_x * gx_count)
    valid_y = real_y & (global_y >= 0) & (global_y < rows_y * gy_count)
    valid = (valid_x[:, None] & valid_y[None, :]).astype(jnp.float32)
    lo = spins_e[:, :1]
    hi = spins_e[:, -1:]
    for sweep_index in range(SWEEPS):
        for colour in (0, 1):
            below = shift_in(hi, "region", True)
            above = shift_in(lo, "region", False)
            spins_e, lo, hi = half_sweep(
                spins_e, below, above, exch_flat, film_e, valid, trials_e, unif_e, sweep_index, colour
            )
    stack_spins = spins_e[:, :, :rows_x, :rows_y]
    averages = stack_spins[:, 0].reshape(3, piece_x, K, piece_y, K).mean(axis=(2, 4))
    gathered = whole_of(averages[None], (("gx_0", "gx_1", "gy_0"), "gy_1"), 0)
    assembled = (
        gathered.reshape(gx_count, gy_count, 3, piece_x, piece_y)
        .transpose(2, 0, 3, 1, 4)
        .reshape(3, gx_count * piece_x, gy_count * piece_y)
    )
    padded_block = jnp.pad(
        assembled,
        (
            (0, 0),
            (0, film_m.shape[1] - assembled.shape[1]),
            (0, film_m.shape[2] - assembled.shape[2]),
        ),
    )
    interface = jnp.where(first_tile, padded_block, 0.0)
    magnet_e = film_e4[:3]
    anis_e = film_e4[3]
    interface_e = jnp.pad(interface, ((0, 0), (film_width, film_width), (film_width, film_width)))
    inner = (slice(None), slice(1, -1), slice(1, -1))
    rate_ring = film_rate(magnet_e[inner], magnet_e, anis_e[1:-1, 1:-1], interface_e[inner])
    predicted = magnet_e[inner] + time_step * rate_ring
    rate_start = rate_ring[inner]
    rate_trial = film_rate(predicted[inner], predicted, film_anis, interface)
    corrected = film_m + 0.5 * time_step * (rate_start + rate_trial)
    return (stack_spins, normalized(corrected))


def solution(mesh):
    finer = Mesh(
        mesh.devices.reshape(mesh.shape["region"], 8, 2, 4, 2),
        ("region", "gx_0", "gx_1", "gy_0", "gy_1"),
    )
    in_specs = (
        P(None, "region", GX, GY),
        P(None, "region", GX, GY),
        P(None, None, "region", GX, GY),
        P(),
        P(None, REGION_GX, GY),
        P(REGION_GX, GY),
    )
    out_specs = (P(None, "region", GX, GY), P(None, REGION_GX, GY))
    return jax.shard_map(body, mesh=finer, in_specs=in_specs, out_specs=out_specs, check_vma=False)
```

```python
import functools

import jax
import jax.numpy as jnp
from jax import lax
from jax.sharding import Mesh
from jax.sharding import PartitionSpec as P
from jax.experimental import pallas as pl
from jax.experimental.pallas import tpu as pltpu

K = 8
SWEEPS = 2
REGION_GX = ("region", "gx_0", "gx_1")
GY = ("gy_0", "gy_1")
GX = ("gx_0", "gx_1")
ALL_AXES = ("region", "gx_0", "gx_1", "gy_0", "gy_1")


coupling_down = 1.0
anisotropy = 0.5
inverse_temp = 2.0
softness = 0.05
step_cone = 0.4
coupling_up = 2.0
damping = 0.1
time_step = 0.05


def with_halo(array, sides, width):
    edges = {}
    for axis, dim in sides:
        count, length = (lax.axis_size(axis), array.shape[dim])
        up = [(i, (i + 1) % count) for i in range(count - 1)]
        last = lax.slice_in_dim(array, length - width, length, axis=dim)
        leading = lax.slice_in_dim(array, 0, width, axis=dim)
        edges[dim] = (
            lax.ppermute(last, axis, up),
            lax.ppermute(leading, axis, [(b, a) for a, b in up]),
        )
    done = []
    for _, dim in sides:
        low, high = edges[dim]
        around = [(width, width) if d in done else (0, 0) for d in range(array.ndim)]
        array = jnp.concatenate([jnp.pad(low, around), array, jnp.pad(high, around)], axis=dim)
        done.append(dim)
    return array


def split_up(array, dim, count):
    shape = array.shape
    parts = array.reshape(*shape[:dim], count, shape[dim] // count, *shape[dim + 1 :])
    return jnp.moveaxis(parts, dim, 0)


def summed_on_arrival(array, axis, dim):
    parts = split_up(array, dim, lax.axis_size(axis))
    arrived = lax.all_to_all(parts, axis, split_axis=0, concat_axis=0, tiled=True)
    return arrived.sum(axis=0)


def summed_rows(array, axes, dim):
    far, near = axes
    own = summed_on_arrival(split_up(array, dim, lax.axis_size(far)), near, dim + 1)
    return jnp.sum(lax.all_to_all(own, far, 0, 0, tiled=True), axis=0)


def picked_on_arrival(array, axis, dim):
    parts = split_up(array, dim, lax.axis_size(axis))
    return lax.all_to_all(parts, axis, split_axis=0, concat_axis=0, tiled=True)[0]


def picked_rows(array, axes, dim):
    far, near = axes
    own = picked_on_arrival(split_up(array, dim, lax.axis_size(far)), near, dim + 1)
    return lax.all_to_all(own, far, 0, 0, tiled=True)[0]


def from_first_region(array):
    count = lax.axis_size("region")
    tile = lax.axis_size(GX) * lax.axis_size(GY)
    total = array
    for region in range(1, count):
        total = total + lax.ppermute(array, ALL_AXES, [(0, region * tile)])
    return total


def picked(array, axis, root):
    return lax.dynamic_index_in_dim(lax.all_gather(array, axis), root, 0, keepdims=False)


def copy_for_each(array, axis):
    count = lax.axis_size(axis)
    return lax.all_to_all(
        jnp.broadcast_to(array[None], (count, *array.shape)), axis, 0, 0, tiled=True
    )


def laid_out(parts, dim):
    shape = list(parts.shape[1:])
    shape[dim] *= parts.shape[0]
    return jnp.moveaxis(parts, 0, dim).reshape(shape)


def whole_of(array, axes, dim):
    far, near = axes
    parts = copy_for_each(copy_for_each(array, far), near)
    return laid_out(parts.swapaxes(0, 1).reshape(-1, *array.shape), dim)


def normalized(vector):
    return vector / jnp.sqrt(jnp.sum(vector * vector, axis=0, keepdims=True))


def apply_kernel(matrix, vector):
    return jnp.stack(
        [
            matrix[component, 0] * vector[0]
            + matrix[component, 1] * vector[1]
            + matrix[component, 2] * vector[2]
            for component in range(3)
        ]
    )


def apply_transposed(matrix, vector):
    return jnp.stack(
        [
            matrix[0, component] * vector[0]
            + matrix[1, component] * vector[1]
            + matrix[2, component] * vector[2]
            for component in range(3)
        ]
    )


def local_field(padded, exch_kernel):
    forward = (padded[:, 2:, 1:-1, 1:-1], padded[:, 1:-1, 2:, 1:-1], padded[:, 1:-1, 1:-1, 2:])
    backward = (padded[:, :-2, 1:-1, 1:-1], padded[:, 1:-1, :-2, 1:-1], padded[:, 1:-1, 1:-1, :-2])
    summed = apply_kernel(exch_kernel[0], forward[0]) + apply_transposed(
        exch_kernel[0], backward[0]
    )
    for direction in (1, 2):
        summed = summed + apply_kernel(exch_kernel[direction], forward[direction])
        summed = summed + apply_transposed(exch_kernel[direction], backward[direction])
    return summed


def metropolis(spins, padded, exch_kernel, film_near, trial_move, uniform_draw, colour_mask):
    field_sum = local_field(padded, exch_kernel) + coupling_down * film_near
    proposal = normalized(spins + step_cone * trial_move)
    change = -jnp.sum((proposal - spins) * field_sum, axis=0) - anisotropy * (
        proposal[2] * proposal[2] - spins[2] * spins[2]
    )
    accept = jnp.exp(jnp.minimum(-inverse_temp * change, 0.0))
    weight = jax.nn.sigmoid((accept - uniform_draw) / softness)
    blended = normalized((1.0 - weight) * spins + weight * proposal)
    return jnp.where(colour_mask[None], blended, spins)


def sweep_kernel(step_ref, k_ref, s_ref, lo_ref, hi_ref, film_ref, valid_ref, trial_ref, unif_ref,
                 out_ref, olo_ref, ohi_ref):
    layers, rows_x, rows_y = s_ref.shape[1:]
    row = lax.broadcasted_iota(jnp.int32, (rows_x, rows_y), 0)
    col = lax.broadcasted_iota(jnp.int32, (rows_x, rows_y), 1)
    live = valid_ref[...] > 0.5
    sweep = step_ref[0]
    colour = step_ref[1]
    kk = [[[k_ref[d * 9 + a * 3 + b] for b in range(3)] for a in range(3)] for d in range(3)]
    for l in range(layers):
        s = [s_ref[c, l] for c in range(3)]
        below = [lo_ref[c, 0] if l == 0 else s_ref[c, l - 1] for c in range(3)]
        above = [hi_ref[c, 0] if l == layers - 1 else s_ref[c, l + 1] for c in range(3)]
        xp = [pltpu.roll(s[c], rows_x - 1, 0) for c in range(3)]
        xm = [pltpu.roll(s[c], 1, 0) for c in range(3)]
        yp = [pltpu.roll(s[c], rows_y - 1, 1) for c in range(3)]
        ym = [pltpu.roll(s[c], 1, 1) for c in range(3)]
        fwd = (above, xp, yp)
        bwd = (below, xm, ym)
        field = []
        for c in range(3):
            total = film_ref[c] * coupling_down
            for d in range(3):
                m = kk[d]
                total = total + (m[c][0] * fwd[d][0] + m[c][1] * fwd[d][1] + m[c][2] * fwd[d][2])
                total = total + (m[0][c] * bwd[d][0] + m[1][c] * bwd[d][1] + m[2][c] * bwd[d][2])
            field.append(total)
        raw = [s[c] + step_cone * trial_ref[sweep, c, l] for c in range(3)]
        norm = jnp.sqrt(raw[0] * raw[0] + raw[1] * raw[1] + raw[2] * raw[2])
        prop = [raw[c] / norm for c in range(3)]
        dot = (prop[0] - s[0]) * field[0] + (prop[1] - s[1]) * field[1] + (prop[2] - s[2]) * field[2]
        change = -dot - anisotropy * (prop[2] * prop[2] - s[2] * s[2])
        accept = jnp.exp(jnp.minimum(-inverse_temp * change, 0.0))
        weight = 1.0 / (1.0 + jnp.exp(-((accept - unif_ref[sweep, l]) / softness)))
        mix = [(1.0 - weight) * s[c] + weight * prop[c] for c in range(3)]
        mnorm = jnp.sqrt(mix[0] * mix[0] + mix[1] * mix[1] + mix[2] * mix[2])
        chosen = (((row + col + l) % 2) == colour) & live
        for c in range(3):
            new = jnp.where(chosen, mix[c] / mnorm, s[c])
            out_ref[c, l] = new
            if l == 0:
                olo_ref[c, 0] = new
            if l == layers - 1:
                ohi_ref[c, 0] = new


def half_sweep(spins, lo, hi, exch_flat, film_e, valid, trials, uniforms, sweep, colour):
    comps, layers, rows_x, rows_y = spins.shape
    vmem = pl.BlockSpec(memory_space=pltpu.VMEM)
    smem = pl.BlockSpec(memory_space=pltpu.SMEM)
    dt = spins.dtype
    face = jax.ShapeDtypeStruct((comps, 1, rows_x, rows_y), dt)
    out_shape = (jax.ShapeDtypeStruct(spins.shape, dt), face, face)
    sites = layers * rows_x * rows_y
    return pl.pallas_call(
        sweep_kernel,
        out_shape=out_shape,
        in_specs=[smem, smem] + [vmem] * 7,
        out_specs=tuple([vmem] * 3),
        cost_estimate=pl.CostEstimate(flops=200 * sites, transcendentals=4 * sites, bytes_accessed=4 * 14 * sites),
    )(jnp.array([sweep, colour], jnp.int32), exch_flat, spins, lo, hi, film_e, valid, trials, uniforms)


def shift_in(array, axis, from_lower):
    count = lax.axis_size(axis)
    up = [(i, i + 1) for i in range(count - 1)]
    return lax.ppermute(array, axis, up if from_lower else [(b, a) for a, b in up])


def packed(*arrays):
    return jnp.concatenate([array.reshape(-1) for array in arrays])


def unpacked(flat, *likes):
    out, at = [], 0
    for like in likes:
        out.append(flat[at : at + like.size].reshape(like.shape))
        at += like.size
    return out


def extended(array, film, width, film_width, wide):
    rows, cols = array.shape[-2:]
    gx_pos = lax.axis_index(GX)
    last = lax.axis_size(GX) - 1
    s_low, f_low = array[..., rows - width :, :], film[:, -film_width:, :]
    s_high, f_high = array[..., :width, :], film[:, :film_width, :]
    below = unpacked(shift_in(packed(s_low, f_low), REGION_GX, True), s_low, f_low)
    above = unpacked(shift_in(packed(s_high, f_high), REGION_GX, False), s_high, f_high)
    array = jnp.concatenate(
        [array, jnp.where(gx_pos == last, 0.0, above[0]), jnp.where(gx_pos == 0, 0.0, below[0])], axis=-2
    )
    film = jnp.concatenate([below[1], film, above[1]], axis=1)
    s_low = jnp.swapaxes(array[..., cols - width :], -1, -2)
    f_low = jnp.swapaxes(film[:, :, -film_width:], -1, -2)
    s_high = jnp.swapaxes(array[..., :width], -1, -2)
    f_high = jnp.swapaxes(film[:, :, :film_width], -1, -2)
    left = unpacked(shift_in(packed(s_low, f_low), GY, True), s_low, f_low)
    right = unpacked(shift_in(packed(s_high, f_high), GY, False), s_high, f_high)
    gap = jnp.zeros(array.shape[:-1] + (wide - cols - 2 * width,), array.dtype)
    array = jnp.concatenate(
        [array, jnp.swapaxes(right[0], -1, -2), gap, jnp.swapaxes(left[0], -1, -2)], axis=-1
    )
    film = jnp.concatenate(
        [jnp.swapaxes(left[1], -1, -2), film, jnp.swapaxes(right[1], -1, -2)], axis=-1
    )
    return array, film


def cells_for_sites(patch, rows_x, rows_y, width, wide):
    inner = jnp.repeat(patch[:, 1:-1], K, axis=1)
    rows = jnp.concatenate(
        [inner, jnp.repeat(patch[:, -1:], width, axis=1), jnp.repeat(patch[:, :1], width, axis=1)], axis=1
    )
    inner = jnp.repeat(rows[:, :, 1:-1], K, axis=2)
    gap = jnp.zeros(rows.shape[:2] + (wide - rows_y - 2 * width,), rows.dtype)
    return jnp.concatenate(
        [inner, jnp.repeat(rows[:, :, -1:], width, axis=2), gap, jnp.repeat(rows[:, :, :1], width, axis=2)],
        axis=2,
    )


def cross_product(left, right):
    return jnp.stack(
        [
            left[1] * right[2] - left[2] * right[1],
            left[2] * right[0] - left[0] * right[2],
            left[0] * right[1] - left[1] * right[0],
        ]
    )


def film_rate(magnet, padded, film_anis, interface):
    laplace_sum = (
        padded[:, 2:, 1:-1]
        + padded[:, :-2, 1:-1]
        + padded[:, 1:-1, 2:]
        + padded[:, 1:-1, :-2]
        - 4.0 * magnet
    )
    field_sum = laplace_sum + coupling_up * interface
    field_sum = jnp.stack([field_sum[0], field_sum[1], field_sum[2] + film_anis * magnet[2]])
    precession = cross_product(magnet, field_sum)
    relaxation = cross_product(magnet, precession)
    return -(precession + damping * relaxation) / (1.0 + damping * damping)


def film_halo(magnet):
    return with_halo(magnet, ((REGION_GX, 1), (GY, 2)), 1)


def body(spins, uniforms, trials, exch_kernel, film_m, film_anis):
    layers_dev = spins.shape[1]
    rows_x = spins.shape[2]
    rows_y = spins.shape[3]
    piece_x = rows_x // K
    piece_y = rows_y // K
    gx_count = lax.axis_size(GX)
    gy_count = lax.axis_size(GY)
    tile_count = gx_count * gy_count
    region_pos = lax.axis_index("region")
    gx_pos = lax.axis_index(GX)
    gy_pos = lax.axis_index(GY)
    first_tile = (region_pos == 0) & (gx_pos == 0) & (gy_pos == 0)
    film_block = film_m[:, : piece_x * gx_count, : piece_y * gy_count]
    stack_spins, unif_all, trial_all = (spins, uniforms, trials)
    assert layers_dev % 2 == 0 and rows_x % 2 == 0 and rows_y % 2 == 0
    width = 2 * SWEEPS
    ext_x = rows_x + 2 * width
    wide = -(-(rows_y + 2 * width) // 128) * 128
    assert ext_x % 2 == 0 and wide % 2 == 0 and width <= K and width <= rows_x and width <= rows_y
    tiles = film_block.reshape(3, gx_count, piece_x, gy_count, piece_y).transpose(1, 3, 0, 2, 4)
    zero_row = jnp.zeros_like(tiles[:1, :, :, :1])
    tiles = jnp.concatenate(
        [
            jnp.concatenate([zero_row, tiles[:-1, :, :, -1:]], axis=0),
            tiles,
            jnp.concatenate([tiles[1:, :, :, :1], zero_row], axis=0),
        ],
        axis=3,
    )
    zero_col = jnp.zeros_like(tiles[:, :1, :, :, :1])
    tiles = jnp.concatenate(
        [
            jnp.concatenate([zero_col, tiles[:, :-1, :, :, -1:]], axis=1),
            tiles,
            jnp.concatenate([tiles[:, 1:, :, :, :1], zero_col], axis=1),
        ],
        axis=4,
    )
    pieces = tiles.reshape(tile_count, 3, piece_x + 2, piece_y + 2)
    pieces = from_first_region(jnp.where(first_tile, pieces, 0.0))
    own_patch = picked_rows(pieces, (("gx_0", "gx_1", "gy_0"), "gy_1"), 0)[0]
    film_e = cells_for_sites(own_patch, rows_x, rows_y, width, wide)
    exch_flat = exch_kernel.reshape(-1)
    channels = jnp.concatenate(
        [stack_spins, trial_all.reshape(-1, layers_dev, rows_x, rows_y), unif_all], axis=0
    )
    film_width = 2
    film_all = jnp.concatenate([film_m, film_anis[None]], axis=0)
    channels, film_e4 = extended(channels, film_all, width, film_width, wide)
    spins_e = channels[:3]
    trials_e = channels[3 : 3 + 3 * SWEEPS].reshape(SWEEPS, 3, layers_dev, ext_x, wide)
    unif_e = channels[3 + 3 * SWEEPS :]
    local_x = jnp.arange(ext_x, dtype=jnp.int32)
    local_x = jnp.where(local_x < rows_x + width, local_x, local_x - ext_x)
    local_y = jnp.arange(wide, dtype=jnp.int32)
    real_y = (local_y < rows_y + width) | (local_y >= wide - width)
    local_y = jnp.where(local_y < rows_y + width, local_y, local_y - wide)
    global_x = gx_pos * rows_x + local_x
    global_y = gy_pos * rows_y + local_y
    valid_x = (global_x >= 0) & (global_x < rows_x * gx_count)
    valid_y = real_y & (global_y >= 0) & (global_y < rows_y * gy_count)
    valid = (valid_x[:, None] & valid_y[None, :]).astype(jnp.float32)
    lo = spins_e[:, :1]
    hi = spins_e[:, -1:]
    for sweep_index in range(SWEEPS):
        for colour in (0, 1):
            below = shift_in(hi, "region", True)
            above = shift_in(lo, "region", False)
            spins_e, lo, hi = half_sweep(
                spins_e, below, above, exch_flat, film_e, valid, trials_e, unif_e, sweep_index, colour
            )
    stack_spins = spins_e[:, :, :rows_x, :rows_y]
    averages = stack_spins[:, 0].reshape(3, piece_x, K, piece_y, K).mean(axis=(2, 4))
    gathered = whole_of(averages[None], (("gx_0", "gx_1", "gy_0"), "gy_1"), 0)
    assembled = (
        gathered.reshape(gx_count, gy_count, 3, piece_x, piece_y)
        .transpose(2, 0, 3, 1, 4)
        .reshape(3, gx_count * piece_x, gy_count * piece_y)
    )
    padded_block = jnp.pad(
        assembled,
        (
            (0, 0),
            (0, film_m.shape[1] - assembled.shape[1]),
            (0, film_m.shape[2] - assembled.shape[2]),
        ),
    )
    interface = jnp.where(first_tile, padded_block, 0.0)
    magnet_e = film_e4[:3]
    anis_e = film_e4[3]
    interface_e = jnp.pad(interface, ((0, 0), (film_width, film_width), (film_width, film_width)))
    inner = (slice(None), slice(1, -1), slice(1, -1))
    rate_ring = film_rate(magnet_e[inner], magnet_e, anis_e[1:-1, 1:-1], interface_e[inner])
    predicted = magnet_e[inner] + time_step * rate_ring
    rate_start = rate_ring[inner]
    rate_trial = film_rate(predicted[inner], predicted, film_anis, interface)
    corrected = film_m + 0.5 * time_step * (rate_start + rate_trial)
    return (stack_spins, normalized(corrected))


def solution(mesh):
    finer = Mesh(
        mesh.devices.reshape(mesh.shape["region"], 8, 2, 4, 2),
        ("region", "gx_0", "gx_1", "gy_0", "gy_1"),
    )
    in_specs = (
        P(None, "region", GX, GY),
        P(None, "region", GX, GY),
        P(None, None, "region", GX, GY),
        P(),
        P(None, REGION_GX, GY),
        P(REGION_GX, GY),
    )
    out_specs = (P(None, "region", GX, GY), P(None, REGION_GX, GY))
    return jax.shard_map(body, mesh=finer, in_specs=in_specs, out_specs=out_specs, check_vma=False)
```

```python
import functools

import jax
import jax.numpy as jnp
from jax import lax
from jax.sharding import Mesh
from jax.sharding import PartitionSpec as P
from jax.experimental import pallas as pl
from jax.experimental.pallas import tpu as pltpu

K = 8
SWEEPS = 2
REGION_GX = ("region", "gx_0", "gx_1")
GY = ("gy_0", "gy_1")
GX = ("gx_0", "gx_1")
ALL_AXES = ("region", "gx_0", "gx_1", "gy_0", "gy_1")


coupling_down = 1.0
anisotropy = 0.5
inverse_temp = 2.0
softness = 0.05
step_cone = 0.4
coupling_up = 2.0
damping = 0.1
time_step = 0.05


def with_halo(array, sides, width):
    edges = {}
    for axis, dim in sides:
        count, length = (lax.axis_size(axis), array.shape[dim])
        up = [(i, (i + 1) % count) for i in range(count - 1)]
        last = lax.slice_in_dim(array, length - width, length, axis=dim)
        leading = lax.slice_in_dim(array, 0, width, axis=dim)
        edges[dim] = (
            lax.ppermute(last, axis, up),
            lax.ppermute(leading, axis, [(b, a) for a, b in up]),
        )
    done = []
    for _, dim in sides:
        low, high = edges[dim]
        around = [(width, width) if d in done else (0, 0) for d in range(array.ndim)]
        array = jnp.concatenate([jnp.pad(low, around), array, jnp.pad(high, around)], axis=dim)
        done.append(dim)
    return array


def split_up(array, dim, count):
    shape = array.shape
    parts = array.reshape(*shape[:dim], count, shape[dim] // count, *shape[dim + 1 :])
    return jnp.moveaxis(parts, dim, 0)


def summed_on_arrival(array, axis, dim):
    parts = split_up(array, dim, lax.axis_size(axis))
    arrived = lax.all_to_all(parts, axis, split_axis=0, concat_axis=0, tiled=True)
    return arrived.sum(axis=0)


def summed_rows(array, axes, dim):
    far, near = axes
    own = summed_on_arrival(split_up(array, dim, lax.axis_size(far)), near, dim + 1)
    return jnp.sum(lax.all_to_all(own, far, 0, 0, tiled=True), axis=0)


def picked_on_arrival(array, axis, dim):
    parts = split_up(array, dim, lax.axis_size(axis))
    return lax.all_to_all(parts, axis, split_axis=0, concat_axis=0, tiled=True)[0]


def picked_rows(array, axes, dim):
    far, near = axes
    own = picked_on_arrival(split_up(array, dim, lax.axis_size(far)), near, dim + 1)
    return lax.all_to_all(own, far, 0, 0, tiled=True)[0]


def from_first_region(array):
    count = lax.axis_size("region")
    tile = lax.axis_size(GX) * lax.axis_size(GY)
    total = array
    for region in range(1, count):
        total = total + lax.ppermute(array, ALL_AXES, [(0, region * tile)])
    return total


def picked(array, axis, root):
    return lax.dynamic_index_in_dim(lax.all_gather(array, axis), root, 0, keepdims=False)


def copy_for_each(array, axis):
    count = lax.axis_size(axis)
    return lax.all_to_all(
        jnp.broadcast_to(array[None], (count, *array.shape)), axis, 0, 0, tiled=True
    )


def laid_out(parts, dim):
    shape = list(parts.shape[1:])
    shape[dim] *= parts.shape[0]
    return jnp.moveaxis(parts, 0, dim).reshape(shape)


def whole_of(array, axes, dim):
    far, near = axes
    parts = copy_for_each(copy_for_each(array, far), near)
    return laid_out(parts.swapaxes(0, 1).reshape(-1, *array.shape), dim)


def normalized(vector):
    return vector / jnp.sqrt(jnp.sum(vector * vector, axis=0, keepdims=True))


def apply_kernel(matrix, vector):
    return jnp.stack(
        [
            matrix[component, 0] * vector[0]
            + matrix[component, 1] * vector[1]
            + matrix[component, 2] * vector[2]
            for component in range(3)
        ]
    )


def apply_transposed(matrix, vector):
    return jnp.stack(
        [
            matrix[0, component] * vector[0]
            + matrix[1, component] * vector[1]
            + matrix[2, component] * vector[2]
            for component in range(3)
        ]
    )


def local_field(padded, exch_kernel):
    forward = (padded[:, 2:, 1:-1, 1:-1], padded[:, 1:-1, 2:, 1:-1], padded[:, 1:-1, 1:-1, 2:])
    backward = (padded[:, :-2, 1:-1, 1:-1], padded[:, 1:-1, :-2, 1:-1], padded[:, 1:-1, 1:-1, :-2])
    summed = apply_kernel(exch_kernel[0], forward[0]) + apply_transposed(
        exch_kernel[0], backward[0]
    )
    for direction in (1, 2):
        summed = summed + apply_kernel(exch_kernel[direction], forward[direction])
        summed = summed + apply_transposed(exch_kernel[direction], backward[direction])
    return summed


def metropolis(spins, padded, exch_kernel, film_near, trial_move, uniform_draw, colour_mask):
    field_sum = local_field(padded, exch_kernel) + coupling_down * film_near
    proposal = normalized(spins + step_cone * trial_move)
    change = -jnp.sum((proposal - spins) * field_sum, axis=0) - anisotropy * (
        proposal[2] * proposal[2] - spins[2] * spins[2]
    )
    accept = jnp.exp(jnp.minimum(-inverse_temp * change, 0.0))
    weight = jax.nn.sigmoid((accept - uniform_draw) / softness)
    blended = normalized((1.0 - weight) * spins + weight * proposal)
    return jnp.where(colour_mask[None], blended, spins)


def sweep_kernel(step_ref, k_ref, s_ref, lo_ref, hi_ref, film_ref, valid_ref, trial_ref, unif_ref,
                 out_ref, olo_ref, ohi_ref):
    layers, rows_x, rows_y = s_ref.shape[1:]
    row = lax.broadcasted_iota(jnp.int32, (rows_x, rows_y), 0)
    col = lax.broadcasted_iota(jnp.int32, (rows_x, rows_y), 1)
    live = valid_ref[...] > 0.5
    sweep = step_ref[0]
    colour = step_ref[1]
    kk = [[[k_ref[d * 9 + a * 3 + b] for b in range(3)] for a in range(3)] for d in range(3)]
    for l in range(layers):
        s = [s_ref[c, l] for c in range(3)]
        below = [lo_ref[c, 0] if l == 0 else s_ref[c, l - 1] for c in range(3)]
        above = [hi_ref[c, 0] if l == layers - 1 else s_ref[c, l + 1] for c in range(3)]
        xp = [pltpu.roll(s[c], rows_x - 1, 0) for c in range(3)]
        xm = [pltpu.roll(s[c], 1, 0) for c in range(3)]
        yp = [pltpu.roll(s[c], rows_y - 1, 1) for c in range(3)]
        ym = [pltpu.roll(s[c], 1, 1) for c in range(3)]
        fwd = (above, xp, yp)
        bwd = (below, xm, ym)
        field = []
        for c in range(3):
            total = film_ref[c] * coupling_down
            for d in range(3):
                m = kk[d]
                total = total + (m[c][0] * fwd[d][0] + m[c][1] * fwd[d][1] + m[c][2] * fwd[d][2])
                total = total + (m[0][c] * bwd[d][0] + m[1][c] * bwd[d][1] + m[2][c] * bwd[d][2])
            field.append(total)
        raw = [s[c] + step_cone * trial_ref[sweep, c, l] for c in range(3)]
        norm = jnp.sqrt(raw[0] * raw[0] + raw[1] * raw[1] + raw[2] * raw[2])
        prop = [raw[c] / norm for c in range(3)]
        dot = (prop[0] - s[0]) * field[0] + (prop[1] - s[1]) * field[1] + (prop[2] - s[2]) * field[2]
        change = -dot - anisotropy * (prop[2] * prop[2] - s[2] * s[2])
        accept = jnp.exp(jnp.minimum(-inverse_temp * change, 0.0))
        weight = 1.0 / (1.0 + jnp.exp(-((accept - unif_ref[sweep, l]) / softness)))
        mix = [(1.0 - weight) * s[c] + weight * prop[c] for c in range(3)]
        mnorm = jnp.sqrt(mix[0] * mix[0] + mix[1] * mix[1] + mix[2] * mix[2])
        chosen = (((row + col + l) % 2) == colour) & live
        for c in range(3):
            new = jnp.where(chosen, mix[c] / mnorm, s[c])
            out_ref[c, l] = new
            if l == 0:
                olo_ref[c, 0] = new
            if l == layers - 1:
                ohi_ref[c, 0] = new


def half_sweep(spins, lo, hi, exch_flat, film_e, valid, trials, uniforms, sweep, colour):
    comps, layers, rows_x, rows_y = spins.shape
    vmem = pl.BlockSpec(memory_space=pltpu.VMEM)
    smem = pl.BlockSpec(memory_space=pltpu.SMEM)
    dt = spins.dtype
    face = jax.ShapeDtypeStruct((comps, 1, rows_x, rows_y), dt)
    out_shape = (jax.ShapeDtypeStruct(spins.shape, dt), face, face)
    sites = layers * rows_x * rows_y
    return pl.pallas_call(
        sweep_kernel,
        out_shape=out_shape,
        in_specs=[smem, smem] + [vmem] * 7,
        out_specs=tuple([vmem] * 3),
        cost_estimate=pl.CostEstimate(flops=200 * sites, transcendentals=4 * sites, bytes_accessed=4 * 14 * sites),
    )(jnp.array([sweep, colour], jnp.int32), exch_flat, spins, lo, hi, film_e, valid, trials, uniforms)


def shift_in(array, axis, from_lower):
    count = lax.axis_size(axis)
    up = [(i, i + 1) for i in range(count - 1)]
    return lax.ppermute(array, axis, up if from_lower else [(b, a) for a, b in up])


def packed(*arrays):
    return jnp.concatenate([array.reshape(-1) for array in arrays])


def unpacked(flat, *likes):
    out, at = [], 0
    for like in likes:
        out.append(flat[at : at + like.size].reshape(like.shape))
        at += like.size
    return out


def extended(array, film, width, film_width, wide):
    rows, cols = array.shape[-2:]
    gx_pos = lax.axis_index(GX)
    last = lax.axis_size(GX) - 1
    s_low, f_low = array[..., rows - width :, :], film[:, -film_width:, :]
    s_high, f_high = array[..., :width, :], film[:, :film_width, :]
    below = unpacked(shift_in(packed(s_low, f_low), REGION_GX, True), s_low, f_low)
    above = unpacked(shift_in(packed(s_high, f_high), REGION_GX, False), s_high, f_high)
    array = jnp.concatenate(
        [array, jnp.where(gx_pos == last, 0.0, above[0]), jnp.where(gx_pos == 0, 0.0, below[0])], axis=-2
    )
    film = jnp.concatenate([below[1], film, above[1]], axis=1)
    s_low = jnp.swapaxes(array[..., cols - width :], -1, -2)
    f_low = jnp.swapaxes(film[:, :, -film_width:], -1, -2)
    s_high = jnp.swapaxes(array[..., :width], -1, -2)
    f_high = jnp.swapaxes(film[:, :, :film_width], -1, -2)
    left = unpacked(shift_in(packed(s_low, f_low), GY, True), s_low, f_low)
    right = unpacked(shift_in(packed(s_high, f_high), GY, False), s_high, f_high)
    gap = jnp.zeros(array.shape[:-1] + (wide - cols - 2 * width,), array.dtype)
    array = jnp.concatenate(
        [array, jnp.swapaxes(right[0], -1, -2), gap, jnp.swapaxes(left[0], -1, -2)], axis=-1
    )
    film = jnp.concatenate(
        [jnp.swapaxes(left[1], -1, -2), film, jnp.swapaxes(right[1], -1, -2)], axis=-1
    )
    return array, film


def cells_for_sites(patch, rows_x, rows_y, width, wide):
    inner = jnp.repeat(patch[:, 1:-1], K, axis=1)
    rows = jnp.concatenate(
        [inner, jnp.repeat(patch[:, -1:], width, axis=1), jnp.repeat(patch[:, :1], width, axis=1)], axis=1
    )
    inner = jnp.repeat(rows[:, :, 1:-1], K, axis=2)
    gap = jnp.zeros(rows.shape[:2] + (wide - rows_y - 2 * width,), rows.dtype)
    return jnp.concatenate(
        [inner, jnp.repeat(rows[:, :, -1:], width, axis=2), gap, jnp.repeat(rows[:, :, :1], width, axis=2)],
        axis=2,
    )


def cross_product(left, right):
    return jnp.stack(
        [
            left[1] * right[2] - left[2] * right[1],
            left[2] * right[0] - left[0] * right[2],
            left[0] * right[1] - left[1] * right[0],
        ]
    )


def film_rate(magnet, padded, film_anis, interface):
    laplace_sum = (
        padded[:, 2:, 1:-1]
        + padded[:, :-2, 1:-1]
        + padded[:, 1:-1, 2:]
        + padded[:, 1:-1, :-2]
        - 4.0 * magnet
    )
    field_sum = laplace_sum + coupling_up * interface
    field_sum = jnp.stack([field_sum[0], field_sum[1], field_sum[2] + film_anis * magnet[2]])
    precession = cross_product(magnet, field_sum)
    relaxation = cross_product(magnet, precession)
    return -(precession + damping * relaxation) / (1.0 + damping * damping)


def film_halo(magnet):
    return with_halo(magnet, ((REGION_GX, 1), (GY, 2)), 1)


def body(spins, uniforms, trials, exch_kernel, film_m, film_anis):
    layers_dev = spins.shape[1]
    rows_x = spins.shape[2]
    rows_y = spins.shape[3]
    piece_x = rows_x // K
    piece_y = rows_y // K
    gx_count = lax.axis_size(GX)
    gy_count = lax.axis_size(GY)
    tile_count = gx_count * gy_count
    region_pos = lax.axis_index("region")
    gx_pos = lax.axis_index(GX)
    gy_pos = lax.axis_index(GY)
    first_tile = (region_pos == 0) & (gx_pos == 0) & (gy_pos == 0)
    film_block = film_m[:, : piece_x * gx_count, : piece_y * gy_count]
    stack_spins, unif_all, trial_all = (spins, uniforms, trials)
    assert layers_dev % 2 == 0 and rows_x % 2 == 0 and rows_y % 2 == 0
    width = 2 * SWEEPS
    ext_x = rows_x + 2 * width
    wide = -(-(rows_y + 2 * width) // 128) * 128
    assert ext_x % 2 == 0 and wide % 2 == 0 and width <= K and width <= rows_x and width <= rows_y
    tiles = film_block.reshape(3, gx_count, piece_x, gy_count, piece_y).transpose(1, 3, 0, 2, 4)
    zero_row = jnp.zeros_like(tiles[:1, :, :, :1])
    tiles = jnp.concatenate(
        [
            jnp.concatenate([zero_row, tiles[:-1, :, :, -1:]], axis=0),
            tiles,
            jnp.concatenate([tiles[1:, :, :, :1], zero_row], axis=0),
        ],
        axis=3,
    )
    zero_col = jnp.zeros_like(tiles[:, :1, :, :, :1])
    tiles = jnp.concatenate(
        [
            jnp.concatenate([zero_col, tiles[:, :-1, :, :, -1:]], axis=1),
            tiles,
            jnp.concatenate([tiles[:, 1:, :, :, :1], zero_col], axis=1),
        ],
        axis=4,
    )
    pieces = tiles.reshape(tile_count, 3, piece_x + 2, piece_y + 2)
    pieces = from_first_region(jnp.where(first_tile, pieces, 0.0))
    own_patch = lax.all_to_all(pieces, GX + GY, 0, 0, tiled=True)[0]
    film_e = cells_for_sites(own_patch, rows_x, rows_y, width, wide)
    exch_flat = exch_kernel.reshape(-1)
    channels = jnp.concatenate(
        [stack_spins, trial_all.reshape(-1, layers_dev, rows_x, rows_y), unif_all], axis=0
    )
    film_width = 2
    film_all = jnp.concatenate([film_m, film_anis[None]], axis=0)
    channels, film_e4 = extended(channels, film_all, width, film_width, wide)
    spins_e = channels[:3]
    trials_e = channels[3 : 3 + 3 * SWEEPS].reshape(SWEEPS, 3, layers_dev, ext_x, wide)
    unif_e = channels[3 + 3 * SWEEPS :]
    local_x = jnp.arange(ext_x, dtype=jnp.int32)
    local_x = jnp.where(local_x < rows_x + width, local_x, local_x - ext_x)
    local_y = jnp.arange(wide, dtype=jnp.int32)
    real_y = (local_y < rows_y + width) | (local_y >= wide - width)
    local_y = jnp.where(local_y < rows_y + width, local_y, local_y - wide)
    global_x = gx_pos * rows_x + local_x
    global_y = gy_pos * rows_y + local_y
    valid_x = (global_x >= 0) & (global_x < rows_x * gx_count)
    valid_y = real_y & (global_y >= 0) & (global_y < rows_y * gy_count)
    valid = (valid_x[:, None] & valid_y[None, :]).astype(jnp.float32)
    lo = spins_e[:, :1]
    hi = spins_e[:, -1:]
    for sweep_index in range(SWEEPS):
        for colour in (0, 1):
            below = shift_in(hi, "region", True)
            above = shift_in(lo, "region", False)
            spins_e, lo, hi = half_sweep(
                spins_e, below, above, exch_flat, film_e, valid, trials_e, unif_e, sweep_index, colour
            )
    stack_spins = spins_e[:, :, :rows_x, :rows_y]
    averages = stack_spins[:, 0].reshape(3, piece_x, K, piece_y, K).mean(axis=(2, 4))
    gathered = copy_for_each(averages, GX + GY)
    assembled = (
        gathered.reshape(gx_count, gy_count, 3, piece_x, piece_y)
        .transpose(2, 0, 3, 1, 4)
        .reshape(3, gx_count * piece_x, gy_count * piece_y)
    )
    padded_block = jnp.pad(
        assembled,
        (
            (0, 0),
            (0, film_m.shape[1] - assembled.shape[1]),
            (0, film_m.shape[2] - assembled.shape[2]),
        ),
    )
    interface = jnp.where(first_tile, padded_block, 0.0)
    magnet_e = film_e4[:3]
    anis_e = film_e4[3]
    interface_e = jnp.pad(interface, ((0, 0), (film_width, film_width), (film_width, film_width)))
    inner = (slice(None), slice(1, -1), slice(1, -1))
    rate_ring = film_rate(magnet_e[inner], magnet_e, anis_e[1:-1, 1:-1], interface_e[inner])
    predicted = magnet_e[inner] + time_step * rate_ring
    rate_start = rate_ring[inner]
    rate_trial = film_rate(predicted[inner], predicted, film_anis, interface)
    corrected = film_m + 0.5 * time_step * (rate_start + rate_trial)
    return (stack_spins, normalized(corrected))


def solution(mesh):
    finer = Mesh(
        mesh.devices.reshape(mesh.shape["region"], 8, 2, 4, 2),
        ("region", "gx_0", "gx_1", "gy_0", "gy_1"),
    )
    in_specs = (
        P(None, "region", GX, GY),
        P(None, "region", GX, GY),
        P(None, None, "region", GX, GY),
        P(),
        P(None, REGION_GX, GY),
        P(REGION_GX, GY),
    )
    out_specs = (P(None, "region", GX, GY), P(None, REGION_GX, GY))
    return jax.shard_map(body, mesh=finer, in_specs=in_specs, out_specs=out_specs, check_vma=False)
```

```python
import functools

import jax
import jax.numpy as jnp
from jax import lax
from jax.sharding import Mesh
from jax.sharding import PartitionSpec as P
from jax.experimental import pallas as pl
from jax.experimental.pallas import tpu as pltpu

K = 8
SWEEPS = 2
REGION_GX = ("region", "gx_0", "gx_1")
GY = ("gy_0", "gy_1")
GX = ("gx_0", "gx_1")
ALL_AXES = ("region", "gx_0", "gx_1", "gy_0", "gy_1")


coupling_down = 1.0
anisotropy = 0.5
inverse_temp = 2.0
softness = 0.05
step_cone = 0.4
coupling_up = 2.0
damping = 0.1
time_step = 0.05


def from_first_region(array):
    count = lax.axis_size("region")
    tile = lax.axis_size(GX) * lax.axis_size(GY)
    total = array
    for region in range(1, count):
        total = total + lax.ppermute(array, ALL_AXES, [(0, region * tile)])
    return total


def copy_for_each(array, axis):
    count = lax.axis_size(axis)
    return lax.all_to_all(
        jnp.broadcast_to(array[None], (count, *array.shape)), axis, 0, 0, tiled=True
    )


def normalized(vector):
    return vector / jnp.sqrt(jnp.sum(vector * vector, axis=0, keepdims=True))


def sweep_kernel(sweep, colour, k_ref, s_ref, lo_ref, hi_ref, film_ref, valid_ref, trial_ref, unif_ref,
                 out_ref, olo_ref, ohi_ref):
    layers, rows_x, rows_y = s_ref.shape[1:]
    row = lax.broadcasted_iota(jnp.int32, (rows_x, rows_y), 0)
    col = lax.broadcasted_iota(jnp.int32, (rows_x, rows_y), 1)
    live = valid_ref[...] > 0.5
    kk = [[[k_ref[d * 9 + a * 3 + b] for b in range(3)] for a in range(3)] for d in range(3)]
    for l in range(layers):
        s = [s_ref[c, l] for c in range(3)]
        below = [lo_ref[c, 0] if l == 0 else s_ref[c, l - 1] for c in range(3)]
        above = [hi_ref[c, 0] if l == layers - 1 else s_ref[c, l + 1] for c in range(3)]
        xp = [pltpu.roll(s[c], rows_x - 1, 0) for c in range(3)]
        xm = [pltpu.roll(s[c], 1, 0) for c in range(3)]
        yp = [pltpu.roll(s[c], rows_y - 1, 1) for c in range(3)]
        ym = [pltpu.roll(s[c], 1, 1) for c in range(3)]
        fwd = (above, xp, yp)
        bwd = (below, xm, ym)
        field = []
        for c in range(3):
            total = film_ref[c] * coupling_down
            for d in range(3):
                m = kk[d]
                total = total + (m[c][0] * fwd[d][0] + m[c][1] * fwd[d][1] + m[c][2] * fwd[d][2])
                total = total + (m[0][c] * bwd[d][0] + m[1][c] * bwd[d][1] + m[2][c] * bwd[d][2])
            field.append(total)
        raw = [s[c] + step_cone * trial_ref[sweep, c, l] for c in range(3)]
        norm = jnp.sqrt(raw[0] * raw[0] + raw[1] * raw[1] + raw[2] * raw[2])
        prop = [raw[c] / norm for c in range(3)]
        dot = (prop[0] - s[0]) * field[0] + (prop[1] - s[1]) * field[1] + (prop[2] - s[2]) * field[2]
        change = -dot - anisotropy * (prop[2] * prop[2] - s[2] * s[2])
        accept = jnp.exp(jnp.minimum(-inverse_temp * change, 0.0))
        weight = 1.0 / (1.0 + jnp.exp(-((accept - unif_ref[sweep, l]) / softness)))
        mix = [(1.0 - weight) * s[c] + weight * prop[c] for c in range(3)]
        mnorm = jnp.sqrt(mix[0] * mix[0] + mix[1] * mix[1] + mix[2] * mix[2])
        chosen = (((row + col + l) % 2) == colour) & live
        for c in range(3):
            new = jnp.where(chosen, mix[c] / mnorm, s[c])
            out_ref[c, l] = new
            if l == 0:
                olo_ref[c, 0] = new
            if l == layers - 1:
                ohi_ref[c, 0] = new


def half_sweep(spins, lo, hi, exch_flat, film_e, valid, trials, uniforms, sweep, colour):
    comps, layers, rows_x, rows_y = spins.shape
    vmem = pl.BlockSpec(memory_space=pltpu.VMEM)
    smem = pl.BlockSpec(memory_space=pltpu.SMEM)
    dt = spins.dtype
    face = jax.ShapeDtypeStruct((comps, 1, rows_x, rows_y), dt)
    out_shape = (jax.ShapeDtypeStruct(spins.shape, dt), face, face)
    sites = layers * rows_x * rows_y
    return pl.pallas_call(
        functools.partial(sweep_kernel, sweep, colour),
        out_shape=out_shape,
        in_specs=[smem] + [vmem] * 7,
        out_specs=tuple([vmem] * 3),
        cost_estimate=pl.CostEstimate(flops=200 * sites, transcendentals=4 * sites, bytes_accessed=4 * 14 * sites),
    )(exch_flat, spins, lo, hi, film_e, valid, trials, uniforms)


def shift_in(array, axis, from_lower):
    count = lax.axis_size(axis)
    up = [(i, i + 1) for i in range(count - 1)]
    return lax.ppermute(array, axis, up if from_lower else [(b, a) for a, b in up])


def packed(*arrays):
    return jnp.concatenate([array.reshape(-1) for array in arrays])


def unpacked(flat, *likes):
    out, at = [], 0
    for like in likes:
        out.append(flat[at : at + like.size].reshape(like.shape))
        at += like.size
    return out


def extended(array, film, width, film_width, wide):
    rows, cols = array.shape[-2:]
    gx_pos = lax.axis_index(GX)
    last = lax.axis_size(GX) - 1
    s_low, f_low = array[..., rows - width :, :], film[:, -film_width:, :]
    s_high, f_high = array[..., :width, :], film[:, :film_width, :]
    below = unpacked(shift_in(packed(s_low, f_low), REGION_GX, True), s_low, f_low)
    above = unpacked(shift_in(packed(s_high, f_high), REGION_GX, False), s_high, f_high)
    array = jnp.concatenate(
        [array, jnp.where(gx_pos == last, 0.0, above[0]), jnp.where(gx_pos == 0, 0.0, below[0])], axis=-2
    )
    film = jnp.concatenate([below[1], film, above[1]], axis=1)
    s_low = jnp.swapaxes(array[..., cols - width :], -1, -2)
    f_low = jnp.swapaxes(film[:, :, -film_width:], -1, -2)
    s_high = jnp.swapaxes(array[..., :width], -1, -2)
    f_high = jnp.swapaxes(film[:, :, :film_width], -1, -2)
    left = unpacked(shift_in(packed(s_low, f_low), GY, True), s_low, f_low)
    right = unpacked(shift_in(packed(s_high, f_high), GY, False), s_high, f_high)
    gap = jnp.zeros(array.shape[:-1] + (wide - cols - 2 * width,), array.dtype)
    array = jnp.concatenate(
        [array, jnp.swapaxes(right[0], -1, -2), gap, jnp.swapaxes(left[0], -1, -2)], axis=-1
    )
    film = jnp.concatenate(
        [jnp.swapaxes(left[1], -1, -2), film, jnp.swapaxes(right[1], -1, -2)], axis=-1
    )
    return array, film


def cells_for_sites(patch, rows_y, width, wide):
    inner = jnp.repeat(patch[:, 1:-1], K, axis=1)
    rows = jnp.concatenate(
        [inner, jnp.repeat(patch[:, -1:], width, axis=1), jnp.repeat(patch[:, :1], width, axis=1)], axis=1
    )
    inner = jnp.repeat(rows[:, :, 1:-1], K, axis=2)
    gap = jnp.zeros(rows.shape[:2] + (wide - rows_y - 2 * width,), rows.dtype)
    return jnp.concatenate(
        [inner, jnp.repeat(rows[:, :, -1:], width, axis=2), gap, jnp.repeat(rows[:, :, :1], width, axis=2)],
        axis=2,
    )


def cross_product(left, right):
    return jnp.stack(
        [
            left[1] * right[2] - left[2] * right[1],
            left[2] * right[0] - left[0] * right[2],
            left[0] * right[1] - left[1] * right[0],
        ]
    )


def film_rate(magnet, padded, film_anis, interface):
    laplace_sum = (
        padded[:, 2:, 1:-1]
        + padded[:, :-2, 1:-1]
        + padded[:, 1:-1, 2:]
        + padded[:, 1:-1, :-2]
        - 4.0 * magnet
    )
    field_sum = laplace_sum + coupling_up * interface
    field_sum = jnp.stack([field_sum[0], field_sum[1], field_sum[2] + film_anis * magnet[2]])
    precession = cross_product(magnet, field_sum)
    relaxation = cross_product(magnet, precession)
    return -(precession + damping * relaxation) / (1.0 + damping * damping)


def step_body(spins, uniforms, trials, exch_kernel, film_m, film_anis):
    layers_dev = spins.shape[1]
    rows_x = spins.shape[2]
    rows_y = spins.shape[3]
    piece_x = rows_x // K
    piece_y = rows_y // K
    gx_count = lax.axis_size(GX)
    gy_count = lax.axis_size(GY)
    tile_count = gx_count * gy_count
    region_pos = lax.axis_index("region")
    gx_pos = lax.axis_index(GX)
    gy_pos = lax.axis_index(GY)
    first_tile = (region_pos == 0) & (gx_pos == 0) & (gy_pos == 0)
    film_block = film_m[:, : piece_x * gx_count, : piece_y * gy_count]
    stack_spins, unif_all, trial_all = (spins, uniforms, trials)
    assert layers_dev % 2 == 0 and rows_x % 2 == 0 and rows_y % 2 == 0
    width = 2 * SWEEPS
    ext_x = rows_x + 2 * width
    wide = -(-(rows_y + 2 * width) // 128) * 128
    assert ext_x % 2 == 0 and wide % 2 == 0 and width <= K and width <= rows_x and width <= rows_y
    tiles = film_block.reshape(3, gx_count, piece_x, gy_count, piece_y).transpose(1, 3, 0, 2, 4)
    zero_row = jnp.zeros_like(tiles[:1, :, :, :1])
    tiles = jnp.concatenate(
        [
            jnp.concatenate([zero_row, tiles[:-1, :, :, -1:]], axis=0),
            tiles,
            jnp.concatenate([tiles[1:, :, :, :1], zero_row], axis=0),
        ],
        axis=3,
    )
    zero_col = jnp.zeros_like(tiles[:, :1, :, :, :1])
    tiles = jnp.concatenate(
        [
            jnp.concatenate([zero_col, tiles[:, :-1, :, :, -1:]], axis=1),
            tiles,
            jnp.concatenate([tiles[:, 1:, :, :, :1], zero_col], axis=1),
        ],
        axis=4,
    )
    pieces = tiles.reshape(tile_count, 3, piece_x + 2, piece_y + 2)
    pieces = from_first_region(jnp.where(first_tile, pieces, 0.0))
    own_patch = lax.all_to_all(pieces, GX + GY, 0, 0, tiled=True)[0]
    film_e = cells_for_sites(own_patch, rows_y, width, wide)
    exch_flat = exch_kernel.reshape(-1)
    channels = jnp.concatenate(
        [stack_spins, trial_all.reshape(-1, layers_dev, rows_x, rows_y), unif_all], axis=0
    )
    film_width = 2
    film_all = jnp.concatenate([film_m, film_anis[None]], axis=0)
    channels, film_e4 = extended(channels, film_all, width, film_width, wide)
    spins_e = channels[:3]
    trials_e = channels[3 : 3 + 3 * SWEEPS].reshape(SWEEPS, 3, layers_dev, ext_x, wide)
    unif_e = channels[3 + 3 * SWEEPS :]
    local_x = jnp.arange(ext_x, dtype=jnp.int32)
    local_x = jnp.where(local_x < rows_x + width, local_x, local_x - ext_x)
    local_y = jnp.arange(wide, dtype=jnp.int32)
    real_y = (local_y < rows_y + width) | (local_y >= wide - width)
    local_y = jnp.where(local_y < rows_y + width, local_y, local_y - wide)
    global_x = gx_pos * rows_x + local_x
    global_y = gy_pos * rows_y + local_y
    valid_x = (global_x >= 0) & (global_x < rows_x * gx_count)
    valid_y = real_y & (global_y >= 0) & (global_y < rows_y * gy_count)
    valid = (valid_x[:, None] & valid_y[None, :]).astype(jnp.float32)
    lo = spins_e[:, :1]
    hi = spins_e[:, -1:]
    for sweep_index in range(SWEEPS):
        for colour in (0, 1):
            below = shift_in(hi, "region", True)
            above = shift_in(lo, "region", False)
            spins_e, lo, hi = half_sweep(
                spins_e, below, above, exch_flat, film_e, valid, trials_e, unif_e, sweep_index, colour
            )
    stack_spins = spins_e[:, :, :rows_x, :rows_y]
    averages = stack_spins[:, 0].reshape(3, piece_x, K, piece_y, K).mean(axis=(2, 4))
    gathered = copy_for_each(averages, GX + GY)
    assembled = (
        gathered.reshape(gx_count, gy_count, 3, piece_x, piece_y)
        .transpose(2, 0, 3, 1, 4)
        .reshape(3, gx_count * piece_x, gy_count * piece_y)
    )
    padded_block = jnp.pad(
        assembled,
        (
            (0, 0),
            (0, film_m.shape[1] - assembled.shape[1]),
            (0, film_m.shape[2] - assembled.shape[2]),
        ),
    )
    interface = jnp.where(first_tile, padded_block, 0.0)
    magnet_e = film_e4[:3]
    anis_e = film_e4[3]
    interface_e = jnp.pad(interface, ((0, 0), (film_width, film_width), (film_width, film_width)))
    inner = (slice(None), slice(1, -1), slice(1, -1))
    rate_ring = film_rate(magnet_e[inner], magnet_e, anis_e[1:-1, 1:-1], interface_e[inner])
    predicted = magnet_e[inner] + time_step * rate_ring
    rate_start = rate_ring[inner]
    rate_trial = film_rate(predicted[inner], predicted, film_anis, interface)
    corrected = film_m + 0.5 * time_step * (rate_start + rate_trial)
    return (stack_spins, normalized(corrected))


def solution(mesh):
    finer = Mesh(
        mesh.devices.reshape(mesh.shape["region"], 8, 2, 4, 2),
        ("region", "gx_0", "gx_1", "gy_0", "gy_1"),
    )
    in_specs = (
        P(None, "region", GX, GY),
        P(None, "region", GX, GY),
        P(None, None, "region", GX, GY),
        P(),
        P(None, REGION_GX, GY),
        P(REGION_GX, GY),
    )
    out_specs = (P(None, "region", GX, GY), P(None, REGION_GX, GY))
    return jax.shard_map(step_body, mesh=finer, in_specs=in_specs, out_specs=out_specs, check_vma=False)
```

```python
import functools

import jax
import jax.numpy as jnp
from jax import lax
from jax.sharding import Mesh
from jax.sharding import PartitionSpec as P
from jax.experimental import pallas as pl
from jax.experimental.pallas import tpu as pltpu

K = 8
SWEEPS = 2
REGION_GX = ("region", "gx_0", "gx_1")
GY = ("gy_0", "gy_1")
GX = ("gx_0", "gx_1")
ALL_AXES = ("region", "gx_0", "gx_1", "gy_0", "gy_1")


coupling_down = 1.0
anisotropy = 0.5
inverse_temp = 2.0
softness = 0.05
step_cone = 0.4
coupling_up = 2.0
damping = 0.1
time_step = 0.05


def from_first_region(array):
    count = lax.axis_size("region")
    tile = lax.axis_size(GX) * lax.axis_size(GY)
    total = array
    for region in range(1, count):
        total = total + lax.ppermute(array, ALL_AXES, [(0, region * tile)])
    return total


def copy_for_each(array, axis):
    count = lax.axis_size(axis)
    return lax.all_to_all(
        jnp.broadcast_to(array[None], (count, *array.shape)), axis, 0, 0, tiled=True
    )


def normalized(vector):
    return vector / jnp.sqrt(jnp.sum(vector * vector, axis=0, keepdims=True))


def updated(s, below, above, film, trial, unif, chosen, kk):
    rows_x, rows_y = s[0].shape
    xp = [pltpu.roll(s[c], rows_x - 1, 0) for c in range(3)]
    xm = [pltpu.roll(s[c], 1, 0) for c in range(3)]
    yp = [pltpu.roll(s[c], rows_y - 1, 1) for c in range(3)]
    ym = [pltpu.roll(s[c], 1, 1) for c in range(3)]
    fwd = (above, xp, yp)
    bwd = (below, xm, ym)
    field = []
    for c in range(3):
        total = film[c] * coupling_down
        for d in range(3):
            m = kk[d]
            total = total + (m[c][0] * fwd[d][0] + m[c][1] * fwd[d][1] + m[c][2] * fwd[d][2])
            total = total + (m[0][c] * bwd[d][0] + m[1][c] * bwd[d][1] + m[2][c] * bwd[d][2])
        field.append(total)
    raw = [s[c] + step_cone * trial[c] for c in range(3)]
    norm = jnp.sqrt(raw[0] * raw[0] + raw[1] * raw[1] + raw[2] * raw[2])
    prop = [raw[c] / norm for c in range(3)]
    dot = (prop[0] - s[0]) * field[0] + (prop[1] - s[1]) * field[1] + (prop[2] - s[2]) * field[2]
    change = -dot - anisotropy * (prop[2] * prop[2] - s[2] * s[2])
    accept = jnp.exp(jnp.minimum(-inverse_temp * change, 0.0))
    weight = 1.0 / (1.0 + jnp.exp(-((accept - unif) / softness)))
    mix = [(1.0 - weight) * s[c] + weight * prop[c] for c in range(3)]
    mnorm = jnp.sqrt(mix[0] * mix[0] + mix[1] * mix[1] + mix[2] * mix[2])
    return [jnp.where(chosen, mix[c] / mnorm, s[c]) for c in range(3)]


def sweep_kernel(sweep, k_ref, edge_ref, s_ref, b_ref, a_ref, film_ref, valid_ref, trial_ref, unif_ref,
                 tb_ref, ta_ref, out_ref):
    layers, rows_x, rows_y = s_ref.shape[1:]
    row = lax.broadcasted_iota(jnp.int32, (rows_x, rows_y), 0)
    col = lax.broadcasted_iota(jnp.int32, (rows_x, rows_y), 1)
    live = valid_ref[...] > 0.5
    kk = [[[k_ref[d * 9 + a * 3 + b] for b in range(3)] for a in range(3)] for d in range(3)]
    film = [film_ref[c] for c in range(3)]
    halo = b_ref.shape[1]
    stack = [[b_ref[c, l] for c in range(3)] for l in range(halo)]
    stack += [[s_ref[c, l] for c in range(3)] for l in range(layers)]
    stack += [[a_ref[c, l] for c in range(3)] for l in range(halo)]
    trial = [[tb_ref[3 * sweep + c] for c in range(3)]]
    trial += [[trial_ref[sweep, c, l] for c in range(3)] for l in range(layers)]
    trial += [[ta_ref[3 * sweep + c] for c in range(3)]]
    unif = [tb_ref[3 * SWEEPS + sweep]] + [unif_ref[sweep, l] for l in range(layers)] + [ta_ref[3 * SWEEPS + sweep]]
    layer_live = [edge_ref[0] > 0.5] + [True] * layers + [edge_ref[1] > 0.5]
    for colour, first, last in ((0, halo - 1, halo + layers + 1), (1, halo, halo + layers)):
        new = list(stack)
        for i in range(first, last):
            parity = ((row + col + (i - halo) + 2) % 2) == colour
            chosen = parity & live & layer_live[i - halo + 1]
            j = i - (halo - 1)
            new[i] = updated(stack[i], stack[i - 1], stack[i + 1], film, trial[j], unif[j], chosen, kk)
        stack = new
    for l in range(layers):
        for c in range(3):
            out_ref[c, l] = stack[halo + l][c]


def sweep_pair(spins, below, above, exch_flat, edge, film_e, valid, trials, uniforms, tb, ta, sweep):
    _, layers, rows_x, rows_y = spins.shape
    vmem = pl.BlockSpec(memory_space=pltpu.VMEM)
    smem = pl.BlockSpec(memory_space=pltpu.SMEM)
    sites = layers * rows_x * rows_y
    return pl.pallas_call(
        functools.partial(sweep_kernel, sweep),
        out_shape=jax.ShapeDtypeStruct(spins.shape, spins.dtype),
        in_specs=[smem, smem] + [vmem] * 9,
        out_specs=vmem,
        cost_estimate=pl.CostEstimate(flops=600 * sites, transcendentals=12 * sites, bytes_accessed=4 * 30 * sites),
    )(exch_flat, edge, spins, below, above, film_e, valid, trials, uniforms, tb, ta)


def shift_in(array, axis, from_lower):
    count = lax.axis_size(axis)
    up = [(i, i + 1) for i in range(count - 1)]
    return lax.ppermute(array, axis, up if from_lower else [(b, a) for a, b in up])


def packed(*arrays):
    return jnp.concatenate([array.reshape(-1) for array in arrays])


def unpacked(flat, *likes):
    out, at = [], 0
    for like in likes:
        out.append(flat[at : at + like.size].reshape(like.shape))
        at += like.size
    return out


def extended(array, film, width, film_width, wide):
    rows, cols = array.shape[-2:]
    gx_pos = lax.axis_index(GX)
    last = lax.axis_size(GX) - 1
    s_low, f_low = array[..., rows - width :, :], film[:, -film_width:, :]
    s_high, f_high = array[..., :width, :], film[:, :film_width, :]
    below = unpacked(shift_in(packed(s_low, f_low), REGION_GX, True), s_low, f_low)
    above = unpacked(shift_in(packed(s_high, f_high), REGION_GX, False), s_high, f_high)
    array = jnp.concatenate(
        [array, jnp.where(gx_pos == last, 0.0, above[0]), jnp.where(gx_pos == 0, 0.0, below[0])], axis=-2
    )
    film = jnp.concatenate([below[1], film, above[1]], axis=1)
    s_low = jnp.swapaxes(array[..., cols - width :], -1, -2)
    f_low = jnp.swapaxes(film[:, :, -film_width:], -1, -2)
    s_high = jnp.swapaxes(array[..., :width], -1, -2)
    f_high = jnp.swapaxes(film[:, :, :film_width], -1, -2)
    left = unpacked(shift_in(packed(s_low, f_low), GY, True), s_low, f_low)
    right = unpacked(shift_in(packed(s_high, f_high), GY, False), s_high, f_high)
    gap = jnp.zeros(array.shape[:-1] + (wide - cols - 2 * width,), array.dtype)
    array = jnp.concatenate(
        [array, jnp.swapaxes(right[0], -1, -2), gap, jnp.swapaxes(left[0], -1, -2)], axis=-1
    )
    film = jnp.concatenate(
        [jnp.swapaxes(left[1], -1, -2), film, jnp.swapaxes(right[1], -1, -2)], axis=-1
    )
    return array, film


def cells_for_sites(patch, rows_y, width, wide):
    inner = jnp.repeat(patch[:, 1:-1], K, axis=1)
    rows = jnp.concatenate(
        [inner, jnp.repeat(patch[:, -1:], width, axis=1), jnp.repeat(patch[:, :1], width, axis=1)], axis=1
    )
    inner = jnp.repeat(rows[:, :, 1:-1], K, axis=2)
    gap = jnp.zeros(rows.shape[:2] + (wide - rows_y - 2 * width,), rows.dtype)
    return jnp.concatenate(
        [inner, jnp.repeat(rows[:, :, -1:], width, axis=2), gap, jnp.repeat(rows[:, :, :1], width, axis=2)],
        axis=2,
    )


def cross_product(left, right):
    return jnp.stack(
        [
            left[1] * right[2] - left[2] * right[1],
            left[2] * right[0] - left[0] * right[2],
            left[0] * right[1] - left[1] * right[0],
        ]
    )


def film_rate(magnet, padded, film_anis, interface):
    laplace_sum = (
        padded[:, 2:, 1:-1]
        + padded[:, :-2, 1:-1]
        + padded[:, 1:-1, 2:]
        + padded[:, 1:-1, :-2]
        - 4.0 * magnet
    )
    field_sum = laplace_sum + coupling_up * interface
    field_sum = jnp.stack([field_sum[0], field_sum[1], field_sum[2] + film_anis * magnet[2]])
    precession = cross_product(magnet, field_sum)
    relaxation = cross_product(magnet, precession)
    return -(precession + damping * relaxation) / (1.0 + damping * damping)


def step_body(spins, uniforms, trials, exch_kernel, film_m, film_anis):
    layers_dev = spins.shape[1]
    rows_x = spins.shape[2]
    rows_y = spins.shape[3]
    piece_x = rows_x // K
    piece_y = rows_y // K
    gx_count = lax.axis_size(GX)
    gy_count = lax.axis_size(GY)
    tile_count = gx_count * gy_count
    region_pos = lax.axis_index("region")
    gx_pos = lax.axis_index(GX)
    gy_pos = lax.axis_index(GY)
    first_tile = (region_pos == 0) & (gx_pos == 0) & (gy_pos == 0)
    film_block = film_m[:, : piece_x * gx_count, : piece_y * gy_count]
    stack_spins, unif_all, trial_all = (spins, uniforms, trials)
    assert layers_dev % 2 == 0 and rows_x % 2 == 0 and rows_y % 2 == 0
    width = 2 * SWEEPS
    ext_x = rows_x + 2 * width
    wide = -(-(rows_y + 2 * width) // 128) * 128
    assert ext_x % 2 == 0 and wide % 2 == 0 and width <= K and width <= rows_x and width <= rows_y
    tiles = film_block.reshape(3, gx_count, piece_x, gy_count, piece_y).transpose(1, 3, 0, 2, 4)
    zero_row = jnp.zeros_like(tiles[:1, :, :, :1])
    tiles = jnp.concatenate(
        [
            jnp.concatenate([zero_row, tiles[:-1, :, :, -1:]], axis=0),
            tiles,
            jnp.concatenate([tiles[1:, :, :, :1], zero_row], axis=0),
        ],
        axis=3,
    )
    zero_col = jnp.zeros_like(tiles[:, :1, :, :, :1])
    tiles = jnp.concatenate(
        [
            jnp.concatenate([zero_col, tiles[:, :-1, :, :, -1:]], axis=1),
            tiles,
            jnp.concatenate([tiles[:, 1:, :, :, :1], zero_col], axis=1),
        ],
        axis=4,
    )
    pieces = tiles.reshape(tile_count, 3, piece_x + 2, piece_y + 2)
    pieces = from_first_region(jnp.where(first_tile, pieces, 0.0))
    own_patch = lax.all_to_all(pieces, GX + GY, 0, 0, tiled=True)[0]
    film_e = cells_for_sites(own_patch, rows_y, width, wide)
    exch_flat = exch_kernel.reshape(-1)
    channels = jnp.concatenate(
        [stack_spins, trial_all.reshape(-1, layers_dev, rows_x, rows_y), unif_all], axis=0
    )
    film_width = 2
    film_all = jnp.concatenate([film_m, film_anis[None]], axis=0)
    channels, film_e4 = extended(channels, film_all, width, film_width, wide)
    spins_e = channels[:3]
    trials_e = channels[3 : 3 + 3 * SWEEPS].reshape(SWEEPS, 3, layers_dev, ext_x, wide)
    unif_e = channels[3 + 3 * SWEEPS :]
    local_x = jnp.arange(ext_x, dtype=jnp.int32)
    local_x = jnp.where(local_x < rows_x + width, local_x, local_x - ext_x)
    local_y = jnp.arange(wide, dtype=jnp.int32)
    real_y = (local_y < rows_y + width) | (local_y >= wide - width)
    local_y = jnp.where(local_y < rows_y + width, local_y, local_y - wide)
    global_x = gx_pos * rows_x + local_x
    global_y = gy_pos * rows_y + local_y
    valid_x = (global_x >= 0) & (global_x < rows_x * gx_count)
    valid_y = real_y & (global_y >= 0) & (global_y < rows_y * gy_count)
    valid = (valid_x[:, None] & valid_y[None, :]).astype(jnp.float32)
    region_count = lax.axis_size("region")
    edge = jnp.stack([region_pos > 0, region_pos < region_count - 1]).astype(jnp.float32)
    draws = jnp.concatenate([trials_e.reshape(3 * SWEEPS, layers_dev, ext_x, wide), unif_e], axis=0)
    tb = shift_in(draws[:, -1], "region", True)
    ta = shift_in(draws[:, 0], "region", False)
    for sweep_index in range(SWEEPS):
        below = shift_in(spins_e, "region", True)
        above = shift_in(spins_e, "region", False)
        spins_e = sweep_pair(
            spins_e, below, above, exch_flat, edge, film_e, valid, trials_e, unif_e, tb, ta, sweep_index
        )
    stack_spins = spins_e[:, :, :rows_x, :rows_y]
    averages = stack_spins[:, 0].reshape(3, piece_x, K, piece_y, K).mean(axis=(2, 4))
    gathered = copy_for_each(averages, GX + GY)
    assembled = (
        gathered.reshape(gx_count, gy_count, 3, piece_x, piece_y)
        .transpose(2, 0, 3, 1, 4)
        .reshape(3, gx_count * piece_x, gy_count * piece_y)
    )
    padded_block = jnp.pad(
        assembled,
        (
            (0, 0),
            (0, film_m.shape[1] - assembled.shape[1]),
            (0, film_m.shape[2] - assembled.shape[2]),
        ),
    )
    interface = jnp.where(first_tile, padded_block, 0.0)
    magnet_e = film_e4[:3]
    anis_e = film_e4[3]
    interface_e = jnp.pad(interface, ((0, 0), (film_width, film_width), (film_width, film_width)))
    inner = (slice(None), slice(1, -1), slice(1, -1))
    rate_ring = film_rate(magnet_e[inner], magnet_e, anis_e[1:-1, 1:-1], interface_e[inner])
    predicted = magnet_e[inner] + time_step * rate_ring
    rate_start = rate_ring[inner]
    rate_trial = film_rate(predicted[inner], predicted, film_anis, interface)
    corrected = film_m + 0.5 * time_step * (rate_start + rate_trial)
    return (stack_spins, normalized(corrected))


def solution(mesh):
    finer = Mesh(
        mesh.devices.reshape(mesh.shape["region"], 8, 2, 4, 2),
        ("region", "gx_0", "gx_1", "gy_0", "gy_1"),
    )
    in_specs = (
        P(None, "region", GX, GY),
        P(None, "region", GX, GY),
        P(None, None, "region", GX, GY),
        P(),
        P(None, REGION_GX, GY),
        P(REGION_GX, GY),
    )
    out_specs = (P(None, "region", GX, GY), P(None, REGION_GX, GY))
    return jax.shard_map(step_body, mesh=finer, in_specs=in_specs, out_specs=out_specs, check_vma=False)
```

```python
import functools

import jax
import jax.numpy as jnp
from jax import lax
from jax.sharding import Mesh
from jax.sharding import PartitionSpec as P
from jax.experimental import pallas as pl
from jax.experimental.pallas import tpu as pltpu

K = 8
SWEEPS = 2
REGION_GX = ("region", "gx_0", "gx_1")
GY = ("gy_0", "gy_1")
GX = ("gx_0", "gx_1")
ALL_AXES = ("region", "gx_0", "gx_1", "gy_0", "gy_1")


coupling_down = 1.0
anisotropy = 0.5
inverse_temp = 2.0
softness = 0.05
step_cone = 0.4
coupling_up = 2.0
damping = 0.1
time_step = 0.05


def from_first_region(array):
    count = lax.axis_size("region")
    tile = lax.axis_size(GX) * lax.axis_size(GY)
    total = array
    for region in range(1, count):
        total = total + lax.ppermute(array, ALL_AXES, [(0, region * tile)])
    return total


def copy_for_each(array, axis):
    count = lax.axis_size(axis)
    return lax.all_to_all(
        jnp.broadcast_to(array[None], (count, *array.shape)), axis, 0, 0, tiled=True
    )


def normalized(vector):
    return vector / jnp.sqrt(jnp.sum(vector * vector, axis=0, keepdims=True))


def updated(s, below, above, film, trial, unif, chosen, kk):
    rows_x, rows_y = s[0].shape
    xp = [pltpu.roll(s[c], rows_x - 1, 0) for c in range(3)]
    xm = [pltpu.roll(s[c], 1, 0) for c in range(3)]
    yp = [pltpu.roll(s[c], rows_y - 1, 1) for c in range(3)]
    ym = [pltpu.roll(s[c], 1, 1) for c in range(3)]
    fwd = (above, xp, yp)
    bwd = (below, xm, ym)
    field = []
    for c in range(3):
        total = film[c] * coupling_down
        for d in range(3):
            m = kk[d]
            total = total + (m[c][0] * fwd[d][0] + m[c][1] * fwd[d][1] + m[c][2] * fwd[d][2])
            total = total + (m[0][c] * bwd[d][0] + m[1][c] * bwd[d][1] + m[2][c] * bwd[d][2])
        field.append(total)
    raw = [s[c] + step_cone * trial[c] for c in range(3)]
    norm = jnp.sqrt(raw[0] * raw[0] + raw[1] * raw[1] + raw[2] * raw[2])
    prop = [raw[c] / norm for c in range(3)]
    dot = (prop[0] - s[0]) * field[0] + (prop[1] - s[1]) * field[1] + (prop[2] - s[2]) * field[2]
    change = -dot - anisotropy * (prop[2] * prop[2] - s[2] * s[2])
    accept = jnp.exp(jnp.minimum(-inverse_temp * change, 0.0))
    weight = 1.0 / (1.0 + jnp.exp(-((accept - unif) / softness)))
    mix = [(1.0 - weight) * s[c] + weight * prop[c] for c in range(3)]
    mnorm = jnp.sqrt(mix[0] * mix[0] + mix[1] * mix[1] + mix[2] * mix[2])
    return [jnp.where(chosen, mix[c] / mnorm, s[c]) for c in range(3)]


def sweep_kernel(sweep, k_ref, edge_ref, s_ref, b_ref, a_ref, film_ref, valid_ref, trial_ref, unif_ref,
                 tb_ref, ta_ref, out_ref):
    layers, rows_x, rows_y = s_ref.shape[1:]
    row = lax.broadcasted_iota(jnp.int32, (rows_x, rows_y), 0)
    col = lax.broadcasted_iota(jnp.int32, (rows_x, rows_y), 1)
    live = valid_ref[...] > 0.5
    kk = [[[k_ref[d * 9 + a * 3 + b] for b in range(3)] for a in range(3)] for d in range(3)]
    film = [film_ref[c] for c in range(3)]
    halo = b_ref.shape[1]
    stack = [[b_ref[c, l] for c in range(3)] for l in range(halo)]
    stack += [[s_ref[c, l] for c in range(3)] for l in range(layers)]
    stack += [[a_ref[c, l] for c in range(3)] for l in range(halo)]
    trial = [[tb_ref[3 * sweep + c] for c in range(3)]]
    trial += [[trial_ref[sweep, c, l] for c in range(3)] for l in range(layers)]
    trial += [[ta_ref[3 * sweep + c] for c in range(3)]]
    unif = [tb_ref[3 * SWEEPS + sweep]] + [unif_ref[sweep, l] for l in range(layers)] + [ta_ref[3 * SWEEPS + sweep]]
    layer_live = [edge_ref[0] > 0.5] + [True] * layers + [edge_ref[1] > 0.5]
    for colour, first, last in ((0, halo - 1, halo + layers + 1), (1, halo, halo + layers)):
        new = list(stack)
        for i in range(first, last):
            parity = ((row + col + (i - halo) + 2) % 2) == colour
            chosen = parity & live & layer_live[i - halo + 1]
            j = i - (halo - 1)
            new[i] = updated(stack[i], stack[i - 1], stack[i + 1], film, trial[j], unif[j], chosen, kk)
        stack = new
    for l in range(layers):
        for c in range(3):
            out_ref[c, l] = stack[halo + l][c]


def sweep_pair(spins, below, above, exch_flat, edge, film_e, valid, trials, uniforms, tb, ta, sweep):
    _, layers, rows_x, rows_y = spins.shape
    vmem = pl.BlockSpec(memory_space=pltpu.VMEM)
    smem = pl.BlockSpec(memory_space=pltpu.SMEM)
    sites = layers * rows_x * rows_y
    return pl.pallas_call(
        functools.partial(sweep_kernel, sweep),
        out_shape=jax.ShapeDtypeStruct(spins.shape, spins.dtype),
        in_specs=[smem, smem] + [vmem] * 9,
        out_specs=vmem,
        cost_estimate=pl.CostEstimate(flops=600 * sites, transcendentals=12 * sites, bytes_accessed=4 * 30 * sites),
    )(exch_flat, edge, spins, below, above, film_e, valid, trials, uniforms, tb, ta)


def shift_in(array, axis, from_lower):
    count = lax.axis_size(axis)
    up = [(i, i + 1) for i in range(count - 1)]
    return lax.ppermute(array, axis, up if from_lower else [(b, a) for a, b in up])


def packed(*arrays):
    return jnp.concatenate([array.reshape(-1) for array in arrays])


def unpacked(flat, *likes):
    out, at = [], 0
    for like in likes:
        out.append(flat[at : at + like.size].reshape(like.shape))
        at += like.size
    return out


def extended(array, film, width, film_width, wide):
    rows, cols = array.shape[-2:]
    gx_pos = lax.axis_index(GX)
    last = lax.axis_size(GX) - 1
    s_low, f_low = array[..., rows - width :, :], film[:, -film_width:, :]
    s_high, f_high = array[..., :width, :], film[:, :film_width, :]
    below = unpacked(shift_in(packed(s_low, f_low), REGION_GX, True), s_low, f_low)
    above = unpacked(shift_in(packed(s_high, f_high), REGION_GX, False), s_high, f_high)
    array = jnp.concatenate(
        [array, jnp.where(gx_pos == last, 0.0, above[0]), jnp.where(gx_pos == 0, 0.0, below[0])], axis=-2
    )
    film = jnp.concatenate([below[1], film, above[1]], axis=1)
    s_low = jnp.swapaxes(array[..., cols - width :], -1, -2)
    f_low = jnp.swapaxes(film[:, :, -film_width:], -1, -2)
    s_high = jnp.swapaxes(array[..., :width], -1, -2)
    f_high = jnp.swapaxes(film[:, :, :film_width], -1, -2)
    left = unpacked(shift_in(packed(s_low, f_low), GY, True), s_low, f_low)
    right = unpacked(shift_in(packed(s_high, f_high), GY, False), s_high, f_high)
    gap = jnp.zeros(array.shape[:-1] + (wide - cols - 2 * width,), array.dtype)
    array = jnp.concatenate(
        [array, jnp.swapaxes(right[0], -1, -2), gap, jnp.swapaxes(left[0], -1, -2)], axis=-1
    )
    film = jnp.concatenate(
        [jnp.swapaxes(left[1], -1, -2), film, jnp.swapaxes(right[1], -1, -2)], axis=-1
    )
    return array, film


def cells_for_sites(patch, rows_y, width, wide):
    inner = jnp.repeat(patch[:, 1:-1], K, axis=1)
    rows = jnp.concatenate(
        [inner, jnp.repeat(patch[:, -1:], width, axis=1), jnp.repeat(patch[:, :1], width, axis=1)], axis=1
    )
    inner = jnp.repeat(rows[:, :, 1:-1], K, axis=2)
    gap = jnp.zeros(rows.shape[:2] + (wide - rows_y - 2 * width,), rows.dtype)
    return jnp.concatenate(
        [inner, jnp.repeat(rows[:, :, -1:], width, axis=2), gap, jnp.repeat(rows[:, :, :1], width, axis=2)],
        axis=2,
    )


def cross_product(left, right):
    return jnp.stack(
        [
            left[1] * right[2] - left[2] * right[1],
            left[2] * right[0] - left[0] * right[2],
            left[0] * right[1] - left[1] * right[0],
        ]
    )


def film_rate(magnet, padded, film_anis, interface):
    laplace_sum = (
        padded[:, 2:, 1:-1]
        + padded[:, :-2, 1:-1]
        + padded[:, 1:-1, 2:]
        + padded[:, 1:-1, :-2]
        - 4.0 * magnet
    )
    field_sum = laplace_sum + coupling_up * interface
    field_sum = jnp.stack([field_sum[0], field_sum[1], field_sum[2] + film_anis * magnet[2]])
    precession = cross_product(magnet, field_sum)
    relaxation = cross_product(magnet, precession)
    return -(precession + damping * relaxation) / (1.0 + damping * damping)


def step_body(spins, uniforms, trials, exch_kernel, film_m, film_anis):
    layers_dev = spins.shape[1]
    rows_x = spins.shape[2]
    rows_y = spins.shape[3]
    piece_x = rows_x // K
    piece_y = rows_y // K
    gx_count = lax.axis_size(GX)
    gy_count = lax.axis_size(GY)
    tile_count = gx_count * gy_count
    region_pos = lax.axis_index("region")
    gx_pos = lax.axis_index(GX)
    gy_pos = lax.axis_index(GY)
    first_tile = (region_pos == 0) & (gx_pos == 0) & (gy_pos == 0)
    film_block = film_m[:, : piece_x * gx_count, : piece_y * gy_count]
    stack_spins, unif_all, trial_all = (spins, uniforms, trials)
    assert layers_dev % 2 == 0 and rows_x % 2 == 0 and rows_y % 2 == 0
    width = 2 * SWEEPS
    ext_x = rows_x + 2 * width
    wide = -(-(rows_y + 2 * width) // 128) * 128
    assert ext_x % 2 == 0 and wide % 2 == 0 and width <= K and width <= rows_x and width <= rows_y
    tiles = film_block.reshape(3, gx_count, piece_x, gy_count, piece_y).transpose(1, 3, 0, 2, 4)
    zero_row = jnp.zeros_like(tiles[:1, :, :, :1])
    tiles = jnp.concatenate(
        [
            jnp.concatenate([zero_row, tiles[:-1, :, :, -1:]], axis=0),
            tiles,
            jnp.concatenate([tiles[1:, :, :, :1], zero_row], axis=0),
        ],
        axis=3,
    )
    zero_col = jnp.zeros_like(tiles[:, :1, :, :, :1])
    tiles = jnp.concatenate(
        [
            jnp.concatenate([zero_col, tiles[:, :-1, :, :, -1:]], axis=1),
            tiles,
            jnp.concatenate([tiles[:, 1:, :, :, :1], zero_col], axis=1),
        ],
        axis=4,
    )
    pieces = tiles.reshape(tile_count, 3, piece_x + 2, piece_y + 2)
    pieces = from_first_region(jnp.where(first_tile, pieces, 0.0))
    own_patch = lax.all_to_all(pieces, GX + GY, 0, 0, tiled=True)[0]
    film_e = cells_for_sites(own_patch, rows_y, width, wide)
    exch_flat = exch_kernel.reshape(-1)
    channels = jnp.concatenate(
        [stack_spins, trial_all.reshape(-1, layers_dev, rows_x, rows_y), unif_all], axis=0
    )
    film_width = 2
    film_all = jnp.concatenate([film_m, film_anis[None]], axis=0)
    channels, film_e4 = extended(channels, film_all, width, film_width, wide)
    spins_e = channels[:3]
    trials_e = channels[3 : 3 + 3 * SWEEPS].reshape(SWEEPS, 3, layers_dev, ext_x, wide)
    unif_e = channels[3 + 3 * SWEEPS :]
    local_x = jnp.arange(ext_x, dtype=jnp.int32)
    local_x = jnp.where(local_x < rows_x + width, local_x, local_x - ext_x)
    local_y = jnp.arange(wide, dtype=jnp.int32)
    real_y = (local_y < rows_y + width) | (local_y >= wide - width)
    local_y = jnp.where(local_y < rows_y + width, local_y, local_y - wide)
    global_x = gx_pos * rows_x + local_x
    global_y = gy_pos * rows_y + local_y
    valid_x = (global_x >= 0) & (global_x < rows_x * gx_count)
    valid_y = real_y & (global_y >= 0) & (global_y < rows_y * gy_count)
    valid = (valid_x[:, None] & valid_y[None, :]).astype(jnp.float32)
    region_count = lax.axis_size("region")
    edge = jnp.stack([region_pos > 0, region_pos < region_count - 1]).astype(jnp.float32)
    draws = jnp.concatenate([trials_e.reshape(3 * SWEEPS, layers_dev, ext_x, wide), unif_e], axis=0)
    block = spins_e.reshape(-1, ext_x, wide)
    below = shift_in(jnp.concatenate([block, draws[:, -1]], axis=0), "region", True)
    above = shift_in(jnp.concatenate([block, draws[:, 0]], axis=0), "region", False)
    tb, ta = below[block.shape[0] :], above[block.shape[0] :]
    below = below[: block.shape[0]].reshape(spins_e.shape)
    above = above[: block.shape[0]].reshape(spins_e.shape)
    for sweep_index in range(SWEEPS):
        if sweep_index > 0:
            below = shift_in(spins_e, "region", True)
            above = shift_in(spins_e, "region", False)
        spins_e = sweep_pair(
            spins_e, below, above, exch_flat, edge, film_e, valid, trials_e, unif_e, tb, ta, sweep_index
        )
    stack_spins = spins_e[:, :, :rows_x, :rows_y]
    averages = stack_spins[:, 0].reshape(3, piece_x, K, piece_y, K).mean(axis=(2, 4))
    gathered = copy_for_each(averages, GX + GY)
    assembled = (
        gathered.reshape(gx_count, gy_count, 3, piece_x, piece_y)
        .transpose(2, 0, 3, 1, 4)
        .reshape(3, gx_count * piece_x, gy_count * piece_y)
    )
    padded_block = jnp.pad(
        assembled,
        (
            (0, 0),
            (0, film_m.shape[1] - assembled.shape[1]),
            (0, film_m.shape[2] - assembled.shape[2]),
        ),
    )
    interface = jnp.where(first_tile, padded_block, 0.0)
    magnet_e = film_e4[:3]
    anis_e = film_e4[3]
    interface_e = jnp.pad(interface, ((0, 0), (film_width, film_width), (film_width, film_width)))
    inner = (slice(None), slice(1, -1), slice(1, -1))
    rate_ring = film_rate(magnet_e[inner], magnet_e, anis_e[1:-1, 1:-1], interface_e[inner])
    predicted = magnet_e[inner] + time_step * rate_ring
    rate_start = rate_ring[inner]
    rate_trial = film_rate(predicted[inner], predicted, film_anis, interface)
    corrected = film_m + 0.5 * time_step * (rate_start + rate_trial)
    return (stack_spins, normalized(corrected))


def solution(mesh):
    finer = Mesh(
        mesh.devices.reshape(mesh.shape["region"], 8, 2, 4, 2),
        ("region", "gx_0", "gx_1", "gy_0", "gy_1"),
    )
    in_specs = (
        P(None, "region", GX, GY),
        P(None, "region", GX, GY),
        P(None, None, "region", GX, GY),
        P(),
        P(None, REGION_GX, GY),
        P(REGION_GX, GY),
    )
    out_specs = (P(None, "region", GX, GY), P(None, REGION_GX, GY))
    return jax.shard_map(step_body, mesh=finer, in_specs=in_specs, out_specs=out_specs, check_vma=False)
```

```python
import functools

import jax
import jax.numpy as jnp
from jax import lax
from jax.sharding import Mesh
from jax.sharding import PartitionSpec as P
from jax.experimental import pallas as pl
from jax.experimental.pallas import tpu as pltpu

K = 8
SWEEPS = 2
REGION_GX = ("region", "gx_0", "gx_1")
GY = ("gy_0", "gy_1")
GX = ("gx_0", "gx_1")
ALL_AXES = ("region", "gx_0", "gx_1", "gy_0", "gy_1")


coupling_down = 1.0
anisotropy = 0.5
inverse_temp = 2.0
softness = 0.05
step_cone = 0.4
coupling_up = 2.0
damping = 0.1
time_step = 0.05


def from_first_region(array):
    count = lax.axis_size("region")
    tile = lax.axis_size(GX) * lax.axis_size(GY)
    total = array
    for region in range(1, count):
        total = total + lax.ppermute(array, ALL_AXES, [(0, region * tile)])
    return total


def copy_for_each(array, axis):
    count = lax.axis_size(axis)
    return lax.all_to_all(
        jnp.broadcast_to(array[None], (count, *array.shape)), axis, 0, 0, tiled=True
    )


def normalized(vector):
    return vector / jnp.sqrt(jnp.sum(vector * vector, axis=0, keepdims=True))


def updated(s, below, above, film, trial, unif, chosen, kk):
    rows_x, rows_y = s[0].shape
    xp = [pltpu.roll(s[c], rows_x - 1, 0) for c in range(3)]
    xm = [pltpu.roll(s[c], 1, 0) for c in range(3)]
    yp = [pltpu.roll(s[c], rows_y - 1, 1) for c in range(3)]
    ym = [pltpu.roll(s[c], 1, 1) for c in range(3)]
    fwd = (above, xp, yp)
    bwd = (below, xm, ym)
    field = []
    for c in range(3):
        total = film[c] * coupling_down
        for d in range(3):
            m = kk[d]
            total = total + (m[c][0] * fwd[d][0] + m[c][1] * fwd[d][1] + m[c][2] * fwd[d][2])
            total = total + (m[0][c] * bwd[d][0] + m[1][c] * bwd[d][1] + m[2][c] * bwd[d][2])
        field.append(total)
    raw = [s[c] + step_cone * trial[c] for c in range(3)]
    norm = jnp.sqrt(raw[0] * raw[0] + raw[1] * raw[1] + raw[2] * raw[2])
    prop = [raw[c] / norm for c in range(3)]
    dot = (prop[0] - s[0]) * field[0] + (prop[1] - s[1]) * field[1] + (prop[2] - s[2]) * field[2]
    change = -dot - anisotropy * (prop[2] * prop[2] - s[2] * s[2])
    accept = jnp.exp(jnp.minimum(-inverse_temp * change, 0.0))
    weight = 1.0 / (1.0 + jnp.exp(-((accept - unif) / softness)))
    mix = [(1.0 - weight) * s[c] + weight * prop[c] for c in range(3)]
    mnorm = jnp.sqrt(mix[0] * mix[0] + mix[1] * mix[1] + mix[2] * mix[2])
    return [jnp.where(chosen, mix[c] / mnorm, s[c]) for c in range(3)]


def sweep_kernel(sweep, k_ref, edge_ref, s_ref, b_ref, a_ref, film_ref, valid_ref, draw_ref,
                 tb_ref, ta_ref, out_ref):
    layers, rows_x, rows_y = s_ref.shape[1:]
    row = lax.broadcasted_iota(jnp.int32, (rows_x, rows_y), 0)
    col = lax.broadcasted_iota(jnp.int32, (rows_x, rows_y), 1)
    live = valid_ref[...] > 0.5
    kk = [[[k_ref[d * 9 + a * 3 + b] for b in range(3)] for a in range(3)] for d in range(3)]
    film = [film_ref[c] for c in range(3)]
    trial_at = 3 + 3 * sweep
    unif_at = 3 + 3 * SWEEPS + sweep
    halo = b_ref.shape[1]
    stack = [[b_ref[c, l] for c in range(3)] for l in range(halo)]
    stack += [[s_ref[c, l] for c in range(3)] for l in range(layers)]
    stack += [[a_ref[c, l] for c in range(3)] for l in range(halo)]
    trial = [[tb_ref[3 * sweep + c] for c in range(3)]]
    trial += [[draw_ref[trial_at + c, l] for c in range(3)] for l in range(layers)]
    trial += [[ta_ref[3 * sweep + c] for c in range(3)]]
    unif = [tb_ref[3 * SWEEPS + sweep]] + [draw_ref[unif_at, l] for l in range(layers)] + [ta_ref[3 * SWEEPS + sweep]]
    layer_live = [edge_ref[0] > 0.5] + [True] * layers + [edge_ref[1] > 0.5]
    for colour, first, last in ((0, halo - 1, halo + layers + 1), (1, halo, halo + layers)):
        new = list(stack)
        for i in range(first, last):
            parity = ((row + col + (i - halo) + 2) % 2) == colour
            chosen = parity & live & layer_live[i - halo + 1]
            j = i - (halo - 1)
            new[i] = updated(stack[i], stack[i - 1], stack[i + 1], film, trial[j], unif[j], chosen, kk)
        stack = new
    for l in range(layers):
        for c in range(3):
            out_ref[c, l] = stack[halo + l][c]


def sweep_pair(spins, below, above, exch_flat, edge, film_e, valid, draws, tb, ta, sweep):
    layers, rows_x, rows_y = spins.shape[1:]
    vmem = pl.BlockSpec(memory_space=pltpu.VMEM)
    smem = pl.BlockSpec(memory_space=pltpu.SMEM)
    sites = layers * rows_x * rows_y
    return pl.pallas_call(
        functools.partial(sweep_kernel, sweep),
        out_shape=jax.ShapeDtypeStruct((3,) + spins.shape[1:], spins.dtype),
        in_specs=[smem, smem] + [vmem] * 8,
        out_specs=vmem,
        cost_estimate=pl.CostEstimate(flops=600 * sites, transcendentals=12 * sites, bytes_accessed=4 * 30 * sites),
    )(exch_flat, edge, spins, below, above, film_e, valid, draws, tb, ta)


def shift_in(array, axis, from_lower):
    count = lax.axis_size(axis)
    up = [(i, i + 1) for i in range(count - 1)]
    return lax.ppermute(array, axis, up if from_lower else [(b, a) for a, b in up])


def packed(*arrays):
    return jnp.concatenate([array.reshape(-1) for array in arrays])


def unpacked(flat, *likes):
    out, at = [], 0
    for like in likes:
        out.append(flat[at : at + like.size].reshape(like.shape))
        at += like.size
    return out


def extended(array, film, width, film_width, wide):
    rows, cols = array.shape[-2:]
    gx_pos = lax.axis_index(GX)
    last = lax.axis_size(GX) - 1
    s_low, f_low = array[..., rows - width :, :], film[:, -film_width:, :]
    s_high, f_high = array[..., :width, :], film[:, :film_width, :]
    below = unpacked(shift_in(packed(s_low, f_low), REGION_GX, True), s_low, f_low)
    above = unpacked(shift_in(packed(s_high, f_high), REGION_GX, False), s_high, f_high)
    array = jnp.concatenate(
        [array, jnp.where(gx_pos == last, 0.0, above[0]), jnp.where(gx_pos == 0, 0.0, below[0])], axis=-2
    )
    film = jnp.concatenate([below[1], film, above[1]], axis=1)
    s_low = jnp.swapaxes(array[..., cols - width :], -1, -2)
    f_low = jnp.swapaxes(film[:, :, -film_width:], -1, -2)
    s_high = jnp.swapaxes(array[..., :width], -1, -2)
    f_high = jnp.swapaxes(film[:, :, :film_width], -1, -2)
    left = unpacked(shift_in(packed(s_low, f_low), GY, True), s_low, f_low)
    right = unpacked(shift_in(packed(s_high, f_high), GY, False), s_high, f_high)
    gap = jnp.zeros(array.shape[:-1] + (wide - cols - 2 * width,), array.dtype)
    array = jnp.concatenate(
        [array, jnp.swapaxes(right[0], -1, -2), gap, jnp.swapaxes(left[0], -1, -2)], axis=-1
    )
    film = jnp.concatenate(
        [jnp.swapaxes(left[1], -1, -2), film, jnp.swapaxes(right[1], -1, -2)], axis=-1
    )
    return array, film


def cells_for_sites(patch, rows_y, width, wide):
    inner = jnp.repeat(patch[:, 1:-1], K, axis=1)
    rows = jnp.concatenate(
        [inner, jnp.repeat(patch[:, -1:], width, axis=1), jnp.repeat(patch[:, :1], width, axis=1)], axis=1
    )
    inner = jnp.repeat(rows[:, :, 1:-1], K, axis=2)
    gap = jnp.zeros(rows.shape[:2] + (wide - rows_y - 2 * width,), rows.dtype)
    return jnp.concatenate(
        [inner, jnp.repeat(rows[:, :, -1:], width, axis=2), gap, jnp.repeat(rows[:, :, :1], width, axis=2)],
        axis=2,
    )


def cross_product(left, right):
    return jnp.stack(
        [
            left[1] * right[2] - left[2] * right[1],
            left[2] * right[0] - left[0] * right[2],
            left[0] * right[1] - left[1] * right[0],
        ]
    )


def film_rate(magnet, padded, film_anis, interface):
    laplace_sum = (
        padded[:, 2:, 1:-1]
        + padded[:, :-2, 1:-1]
        + padded[:, 1:-1, 2:]
        + padded[:, 1:-1, :-2]
        - 4.0 * magnet
    )
    field_sum = laplace_sum + coupling_up * interface
    field_sum = jnp.stack([field_sum[0], field_sum[1], field_sum[2] + film_anis * magnet[2]])
    precession = cross_product(magnet, field_sum)
    relaxation = cross_product(magnet, precession)
    return -(precession + damping * relaxation) / (1.0 + damping * damping)


def step_body(spins, uniforms, trials, exch_kernel, film_m, film_anis):
    layers_dev = spins.shape[1]
    rows_x = spins.shape[2]
    rows_y = spins.shape[3]
    piece_x = rows_x // K
    piece_y = rows_y // K
    gx_count = lax.axis_size(GX)
    gy_count = lax.axis_size(GY)
    tile_count = gx_count * gy_count
    region_pos = lax.axis_index("region")
    gx_pos = lax.axis_index(GX)
    gy_pos = lax.axis_index(GY)
    first_tile = (region_pos == 0) & (gx_pos == 0) & (gy_pos == 0)
    film_block = film_m[:, : piece_x * gx_count, : piece_y * gy_count]
    stack_spins, unif_all, trial_all = (spins, uniforms, trials)
    assert layers_dev % 2 == 0 and rows_x % 2 == 0 and rows_y % 2 == 0
    width = 2 * SWEEPS
    ext_x = rows_x + 2 * width
    wide = -(-(rows_y + 2 * width) // 128) * 128
    assert ext_x % 2 == 0 and wide % 2 == 0 and width <= K and width <= rows_x and width <= rows_y
    tiles = film_block.reshape(3, gx_count, piece_x, gy_count, piece_y).transpose(1, 3, 0, 2, 4)
    zero_row = jnp.zeros_like(tiles[:1, :, :, :1])
    tiles = jnp.concatenate(
        [
            jnp.concatenate([zero_row, tiles[:-1, :, :, -1:]], axis=0),
            tiles,
            jnp.concatenate([tiles[1:, :, :, :1], zero_row], axis=0),
        ],
        axis=3,
    )
    zero_col = jnp.zeros_like(tiles[:, :1, :, :, :1])
    tiles = jnp.concatenate(
        [
            jnp.concatenate([zero_col, tiles[:, :-1, :, :, -1:]], axis=1),
            tiles,
            jnp.concatenate([tiles[:, 1:, :, :, :1], zero_col], axis=1),
        ],
        axis=4,
    )
    pieces = tiles.reshape(tile_count, 3, piece_x + 2, piece_y + 2)
    pieces = from_first_region(jnp.where(first_tile, pieces, 0.0))
    own_patch = lax.all_to_all(pieces, GX + GY, 0, 0, tiled=True)[0]
    film_e = cells_for_sites(own_patch, rows_y, width, wide)
    exch_flat = exch_kernel.reshape(-1)
    channels = jnp.concatenate(
        [stack_spins, trial_all.reshape(-1, layers_dev, rows_x, rows_y), unif_all], axis=0
    )
    film_width = 2
    film_all = jnp.concatenate([film_m, film_anis[None]], axis=0)
    channels, film_e4 = extended(channels, film_all, width, film_width, wide)
    spins_e = channels[:3]
    trials_e = channels[3 : 3 + 3 * SWEEPS].reshape(SWEEPS, 3, layers_dev, ext_x, wide)
    unif_e = channels[3 + 3 * SWEEPS :]
    local_x = jnp.arange(ext_x, dtype=jnp.int32)
    local_x = jnp.where(local_x < rows_x + width, local_x, local_x - ext_x)
    local_y = jnp.arange(wide, dtype=jnp.int32)
    real_y = (local_y < rows_y + width) | (local_y >= wide - width)
    local_y = jnp.where(local_y < rows_y + width, local_y, local_y - wide)
    global_x = gx_pos * rows_x + local_x
    global_y = gy_pos * rows_y + local_y
    valid_x = (global_x >= 0) & (global_x < rows_x * gx_count)
    valid_y = real_y & (global_y >= 0) & (global_y < rows_y * gy_count)
    valid = (valid_x[:, None] & valid_y[None, :]).astype(jnp.float32)
    region_count = lax.axis_size("region")
    edge = jnp.stack([region_pos > 0, region_pos < region_count - 1]).astype(jnp.float32)
    draws = jnp.concatenate([trials_e.reshape(3 * SWEEPS, layers_dev, ext_x, wide), unif_e], axis=0)
    tb = shift_in(draws[:, -1], "region", True)
    ta = shift_in(draws[:, 0], "region", False)
    current = channels
    for sweep_index in range(SWEEPS):
        below = shift_in(spins_e, "region", True)
        above = shift_in(spins_e, "region", False)
        spins_e = sweep_pair(
            current, below, above, exch_flat, edge, film_e, valid, channels, tb, ta, sweep_index
        )
        current = spins_e
    stack_spins = spins_e[:, :, :rows_x, :rows_y]
    averages = stack_spins[:, 0].reshape(3, piece_x, K, piece_y, K).mean(axis=(2, 4))
    gathered = copy_for_each(averages, GX + GY)
    assembled = (
        gathered.reshape(gx_count, gy_count, 3, piece_x, piece_y)
        .transpose(2, 0, 3, 1, 4)
        .reshape(3, gx_count * piece_x, gy_count * piece_y)
    )
    padded_block = jnp.pad(
        assembled,
        (
            (0, 0),
            (0, film_m.shape[1] - assembled.shape[1]),
            (0, film_m.shape[2] - assembled.shape[2]),
        ),
    )
    interface = jnp.where(first_tile, padded_block, 0.0)
    magnet_e = film_e4[:3]
    anis_e = film_e4[3]
    interface_e = jnp.pad(interface, ((0, 0), (film_width, film_width), (film_width, film_width)))
    inner = (slice(None), slice(1, -1), slice(1, -1))
    rate_ring = film_rate(magnet_e[inner], magnet_e, anis_e[1:-1, 1:-1], interface_e[inner])
    predicted = magnet_e[inner] + time_step * rate_ring
    rate_start = rate_ring[inner]
    rate_trial = film_rate(predicted[inner], predicted, film_anis, interface)
    corrected = film_m + 0.5 * time_step * (rate_start + rate_trial)
    return (stack_spins, normalized(corrected))


def solution(mesh):
    finer = Mesh(
        mesh.devices.reshape(mesh.shape["region"], 8, 2, 4, 2),
        ("region", "gx_0", "gx_1", "gy_0", "gy_1"),
    )
    in_specs = (
        P(None, "region", GX, GY),
        P(None, "region", GX, GY),
        P(None, None, "region", GX, GY),
        P(),
        P(None, REGION_GX, GY),
        P(REGION_GX, GY),
    )
    out_specs = (P(None, "region", GX, GY), P(None, REGION_GX, GY))
    return jax.shard_map(step_body, mesh=finer, in_specs=in_specs, out_specs=out_specs, check_vma=False)
```
